32 devices in a mesh: groups: 2 (over x), wide: 16 (over z, y, core).
Axes of the slice: x: 2, y: 2, z: 4, core: 2. Of those that a mesh axis runs over, the one named last changes fastest.
Arguments:
- retarded_tiles: bfloat16 [32, 16, 2, 128, 128], P(('groups', 'wide')), parts along dimension 0, may hold values from -0.0625 to 0.0625
- tile_lags: int32 [32, 16, 2], P(('groups', 'wide')), parts along dimension 0, may hold values from 1 to 4, as said below
- block_owner: int32 [32], P('groups'), parts along dimension 0, may hold values from 0 to 15, each once
- later_current: bfloat16 [4, 4096, 128], P(None, ('groups', 'wide')), parts along dimension 1, may hold values from -6 to 6
- excitation: float32 [3, 4096, 128], P(None, ('groups', 'wide')), parts along dimension 1, may hold values from -6 to 6
- inverse_blocks: float32 [32, 128, 128], P(('groups', 'wide')), parts along dimension 0, may hold values from -0.5 to 0.5
Outputs:
- adjoint_current: float32 [3, 4096, 128], P(None, ('groups', 'wide')), parts along dimension 1
The draws below stay inside these ranges and needn't reach their ends.
There are 2 independent parts, one for each index of `groups`. The reference program is written for one: setup_inputs(seed, part) draws one part's arguments, and reference() takes and returns one part's arrays. A program takes and returns all parts, laid end to end along the dimension named above; each array names one. Nothing has to cross between parts.
Inputs may be any that keep to these rules, and one draw needn't show every extreme that they name: `tile_lags`: the two slots of every tile name different lags. `block_owner`: each edge block is named once.
All inputs are finite; a program needn't handle non-finite values.
Results may differ from the reference program's by a relative error of at most 0.003.
Values may be sent and summed in bfloat16 or wider, within the bound.
No kernel may reach another device: no remote copies, remote signals or barrier semaphores. Data moves between devices by JAX's collectives and lax.ppermute only.
A program may use at most 128 MiB of HBM per device.

```python
import jax
import jax.numpy as jnp
from jax import lax

TILE = 128
PULSES = 128
STEPS = 3
LAGS = 4
NBLK = 16
EDGES = 2048


def draw_tile_lags(key, part):
    first_key = jax.random.fold_in(key, 11)
    second_key = jax.random.fold_in(key, 23)
    first = jax.random.randint(first_key, (NBLK, NBLK), 0, 4)
    offset = jax.random.randint(second_key, (NBLK, NBLK), 1, 4)
    second = (first + offset) % 4
    return (jnp.stack([first, second], axis=-1) + 1).astype(jnp.int32)


def level_of(rng, extent, pieces, least, largest):
    level, own = 1.0, jax.random.fold_in(rng, 6)
    for dim, shards_of in pieces:
        heights = jnp.exp(jax.random.uniform(jax.random.fold_in(own, dim), (shards_of,), jnp.float32, least / len(pieces), largest / len(pieces)))
        level = level * jnp.repeat(heights, extent[dim] // shards_of).reshape([-1 if axis == dim else 1 for axis in range(len(extent))])
    return level


def normal_values(rng, shape, scale, limit, cuts=(), kind=jnp.bfloat16):
    array = scale * jax.random.normal(rng, shape, jnp.float32)
    if cuts:
        array = array * level_of(rng, shape, cuts, -0.22, 0.18)
    return jnp.clip(array, -limit, limit).astype(kind)


def setup_inputs(seed: int = 0, part: int = 0) -> dict:
    arg_keys = jax.random.split(jax.random.key(seed), 7)
    own_keys = jax.random.split(jax.random.fold_in(arg_keys[6], part), 7)
    return {
        "retarded_tiles": normal_values(own_keys[0], (NBLK, NBLK, 2, TILE, TILE), (4 * EDGES) ** -0.5, 0.0625, ((0, 16),)),
        "tile_lags": draw_tile_lags(jax.random.fold_in(jax.random.fold_in(arg_keys[6], part), 71), part),
        "block_owner": jax.random.permutation(own_keys[2], NBLK).astype(jnp.int32),
        "later_current": normal_values(own_keys[3], (LAGS, EDGES, PULSES), 1.0, 6.0, ((1, 16),)),
        "excitation": normal_values(own_keys[4], (STEPS, EDGES, PULSES), 1.0, 6.0, ((1, 16),), jnp.float32),
        "inverse_blocks": normal_values(own_keys[5], (NBLK, TILE, TILE), TILE ** -0.5, 0.5, ((0, 16),), jnp.float32),
    }


def reference(retarded_tiles, tile_lags, block_owner, later_current, excitation, inverse_blocks):
    history = {}
    for offset in range(LAGS):
        history[STEPS + offset] = later_current[offset].reshape(NBLK, TILE, PULSES)
    results = [None] * STEPS
    for moment in range(STEPS - 1, -1, -1):
        stacked = jnp.stack([history[moment + delay + 1] for delay in range(LAGS)])
        stacked = jnp.take(stacked, block_owner.astype(jnp.int32), axis=1)

        def one_row(pair):
            tiles_row, lags_row = pair
            chosen = jnp.zeros((NBLK, 2, TILE, PULSES), jnp.bfloat16)
            for delay in range(LAGS):
                chosen = jnp.where((lags_row == delay + 1)[:, :, None, None], stacked[delay][:, None], chosen)
            return jnp.einsum('jspq,jspr->qr', tiles_row.astype(jnp.float32), chosen.astype(jnp.float32))

        retarded = lax.map(one_row, (retarded_tiles, tile_lags))
        source = excitation[moment].reshape(NBLK, TILE, PULSES) - retarded
        current = jnp.einsum('ipq,ipr->iqr', inverse_blocks, source, precision=lax.Precision.HIGHEST)
        results[moment] = current.reshape(EDGES, PULSES)
        history[moment] = current.astype(jnp.bfloat16)
    return jnp.stack(results)
```

```python
import functools

import jax
import jax.numpy as jnp
from jax import lax
from jax.sharding import PartitionSpec as P


def inner_size(wide):
    for size in (4, 2):
        if wide % size == 0:
            return size
    return 1


def gather_lines_first(x, wide, inner):
    lines = wide // inner
    line_groups = [[z * inner + k for z in range(lines)] for k in range(inner)]
    along = lax.all_gather(x, "wide", axis=0, tiled=False, axis_index_groups=line_groups)
    parts = [along]
    for m in range(1, inner):
        parts.append(lax.ppermute(along, "wide", [(d, d ^ m) for d in range(wide)]))
    return jnp.stack(parts).reshape((wide,) + x.shape)


def rowwise(tiles, currents):
    spec = "slpq,slpr->qr" if tiles.ndim == 4 else "spq,spr->qr"
    return jnp.einsum(spec, tiles, currents, preferred_element_type=jnp.float32)


def per_device(wide, retarded_tiles, tile_lags, block_owner, later_current, excitation, inverse_blocks):
    inner = inner_size(wide)
    lines = wide // inner
    lag_count = later_current.shape[0]
    step_count = excitation.shape[0]
    me = lax.axis_index("wide")
    own = me % inner

    slot = jnp.arange(wide, dtype=jnp.int32)
    slot_block = (slot % lines) * inner + jnp.bitwise_xor(own, slot // lines)
    block = jnp.arange(wide, dtype=jnp.int32)
    block_slot = jnp.bitwise_xor(block % inner, own) * lines + block // inner

    column_of_block = jnp.argsort(block_owner)
    column_of_slot = jnp.take(column_of_block, slot_block, axis=0)
    tiles = jnp.take(retarded_tiles[0], column_of_slot, axis=0)
    lags = jnp.take(tile_lags[0], column_of_slot, axis=0)

    zero = jnp.zeros_like(tiles[:, 0])
    by_lag = jnp.stack(
        [
            jnp.where(
                (lags[:, 0] == lag)[:, None, None],
                tiles[:, 0],
                jnp.where((lags[:, 1] == lag)[:, None, None], tiles[:, 1], zero),
            )
            for lag in range(1, lag_count + 1)
        ],
        axis=1,
    )

    later = gather_lines_first(later_current, wide, inner)
    inverse_t = inverse_blocks[0].T

    def advance(moment, retarded):
        source = excitation[moment] - retarded
        return jnp.dot(
            inverse_t, source, precision=lax.Precision.HIGHEST, preferred_element_type=jnp.float32
        )

    by_block = jnp.take(by_lag[:, :2], block_slot, axis=0)

    results = [None] * step_count
    newer = {}
    for moment in range(step_count - 1, -1, -1):
        known = [
            delay for delay in range(1, lag_count + 1) if moment + delay >= step_count
        ]
        first = known[0]
        retarded = rowwise(
            by_lag[:, first - 1 :],
            later[:, moment + first - step_count : moment + lag_count + 1 - step_count],
        )
        for delay in range(1, first):
            retarded = retarded + rowwise(by_block[:, delay - 1], newer[moment + delay])
        current = advance(moment, retarded)
        results[moment] = current
        if moment > 0:
            newer[moment] = lax.all_gather(
                current.astype(jnp.bfloat16), "wide", axis=0, tiled=False
            )
    return jnp.stack(results)


def solution(mesh):
    in_specs = (
        P(("groups", "wide"), None, None, None, None),
        P(("groups", "wide"), None, None),
        P("groups"),
        P(None, ("groups", "wide"), None),
        P(None, ("groups", "wide"), None),
        P(("groups", "wide"), None, None),
    )
    out_specs = P(None, ("groups", "wide"), None)
    return jax.shard_map(
        functools.partial(per_device, mesh.shape["wide"]), mesh=mesh, in_specs=in_specs, out_specs=out_specs, check_vma=False
    )
```

```python
import functools

import jax
import jax.numpy as jnp
import numpy as np
from jax import lax
from jax.sharding import PartitionSpec as P


def inner_size(wide):
    for size in (4, 2):
        if wide % size == 0:
            return size
    return 1


def line_stage(x, wide, inner):
    lines = wide // inner
    if lines <= 4:
        parts = [x]
        for shift in range(1, lines):
            pairs = [
                (d, ((d // inner + shift) % lines) * inner + d % inner) for d in range(wide)
            ]
            parts.append(lax.ppermute(x, "wide", pairs))
        return jnp.stack(parts), True
    groups = [[z * inner + k for z in range(lines)] for k in range(inner)]
    return lax.all_gather(x, "wide", axis=0, tiled=False, axis_index_groups=groups), False


def slab_stage(stack, wide, inner, doubling):
    if doubling:
        masks = np.zeros((1,), np.int32)
        bit = inner // 2
        while bit >= 1:
            other = lax.ppermute(stack, "wide", [(d, d ^ bit) for d in range(wide)])
            stack = jnp.stack([stack, other])
            masks = np.concatenate([masks, masks ^ bit])
            bit //= 2
        return stack, masks
    parts = [stack]
    for m in range(1, inner):
        parts.append(lax.ppermute(stack, "wide", [(d, d ^ m) for d in range(wide)]))
    return jnp.stack(parts), np.arange(inner, dtype=np.int32)


def gather_blocks(x, wide, doubling):
    inner = inner_size(wide)
    lines = wide // inner
    stack, shifted = line_stage(x, wide, inner)
    stack, masks = slab_stage(stack, wide, inner, doubling)
    me = lax.axis_index("wide")
    line = np.arange(lines, dtype=np.int32)
    source_line = (me // inner - line) % lines if shifted else jnp.asarray(line)
    blocks = (
        source_line[None, :] * inner
        + jnp.bitwise_xor(me % inner, jnp.asarray(masks))[:, None]
    )
    return stack.reshape((wide,) + x.shape), blocks.reshape(wide)


def tiles_by_lag(retarded_tiles, tile_lags, column_of_block, block_of_slot, lags_wanted):
    columns = jnp.take(column_of_block, block_of_slot, axis=0)
    tiles = jnp.take(retarded_tiles[0], columns, axis=0)
    lags = jnp.take(tile_lags[0], columns, axis=0)
    zero = jnp.zeros_like(tiles[:, 0])
    return jnp.stack(
        [
            jnp.where(
                (lags[:, 0] == lag)[:, None, None],
                tiles[:, 0],
                jnp.where((lags[:, 1] == lag)[:, None, None], tiles[:, 1], zero),
            )
            for lag in lags_wanted
        ],
        axis=1,
    )


def rowwise(tiles, currents):
    spec = "slpq,slpr->qr" if tiles.ndim == 4 else "spq,spr->qr"
    return jnp.einsum(spec, tiles, currents, preferred_element_type=jnp.float32)


def per_device(wide, retarded_tiles, tile_lags, block_owner, later_current, excitation, inverse_blocks):
    lag_count = later_current.shape[0]
    step_count = excitation.shape[0]
    column_of_block = jnp.argsort(block_owner)

    later, later_blocks = gather_blocks(later_current, wide, True)
    by_lag = tiles_by_lag(
        retarded_tiles, tile_lags, column_of_block, later_blocks, range(1, lag_count + 1)
    )
    inverse_t = inverse_blocks[0].T

    def advance(moment, retarded):
        source = excitation[moment] - retarded
        return jnp.dot(
            inverse_t, source, precision=lax.Precision.HIGHEST, preferred_element_type=jnp.float32
        )

    results = [None] * step_count
    newer = {}
    recent = None
    for moment in range(step_count - 1, -1, -1):
        first = max(1, step_count - moment)
        retarded = rowwise(
            by_lag[:, first - 1 :],
            later[:, moment + first - step_count : moment + lag_count + 1 - step_count],
        )
        for delay in range(1, first):
            retarded = retarded + rowwise(recent[:, delay - 1], newer[moment + delay])
        current = advance(moment, retarded)
        results[moment] = current
        if moment > 0:
            newer[moment], new_blocks = gather_blocks(current.astype(jnp.bfloat16), wide, False)
            if recent is None:
                recent = tiles_by_lag(
                    retarded_tiles,
                    tile_lags,
                    column_of_block,
                    new_blocks,
                    range(1, min(lag_count, step_count - 1) + 1),
                )
    return jnp.stack(results)


def solution(mesh):
    in_specs = (
        P(("groups", "wide"), None, None, None, None),
        P(("groups", "wide"), None, None),
        P("groups"),
        P(None, ("groups", "wide"), None),
        P(None, ("groups", "wide"), None),
        P(("groups", "wide"), None, None),
    )
    out_specs = P(None, ("groups", "wide"), None)
    return jax.shard_map(
        functools.partial(per_device, mesh.shape["wide"]),
        mesh=mesh,
        in_specs=in_specs,
        out_specs=out_specs,
        check_vma=False,
    )
```

```python
import functools

import jax
import jax.numpy as jnp
import numpy as np
from jax import lax
from jax.sharding import PartitionSpec as P


def inner_size(wide):
    for size in (4, 2):
        if wide % size == 0:
            return size
    return 1


def line_stage(x, wide, inner):
    lines = wide // inner
    if lines <= 4:
        parts = [x]
        for shift in range(1, lines):
            pairs = [
                (d, ((d // inner + shift) % lines) * inner + d % inner) for d in range(wide)
            ]
            parts.append(lax.ppermute(x, "wide", pairs))
        return jnp.stack(parts), True
    groups = [[z * inner + k for z in range(lines)] for k in range(inner)]
    return lax.all_gather(x, "wide", axis=0, tiled=False, axis_index_groups=groups), False


def slab_stage(stack, wide, inner, doubling):
    if doubling:
        masks = np.zeros((1,), np.int32)
        bit = inner // 2
        while bit >= 1:
            other = lax.ppermute(stack, "wide", [(d, d ^ bit) for d in range(wide)])
            stack = jnp.stack([stack, other])
            masks = np.concatenate([masks, masks ^ bit])
            bit //= 2
        return stack, masks
    parts = [stack]
    for m in range(1, inner):
        parts.append(lax.ppermute(stack, "wide", [(d, d ^ m) for d in range(wide)]))
    return jnp.stack(parts), np.arange(inner, dtype=np.int32)


def gather_blocks(x, wide, doubling):
    inner = inner_size(wide)
    lines = wide // inner
    stack, shifted = line_stage(x, wide, inner)
    stack, masks = slab_stage(stack, wide, inner, doubling)
    me = lax.axis_index("wide")
    line = np.arange(lines, dtype=np.int32)
    source_line = (me // inner - line) % lines if shifted else jnp.asarray(line)
    blocks = (
        source_line[None, :] * inner
        + jnp.bitwise_xor(me % inner, jnp.asarray(masks))[:, None]
    )
    return stack.reshape((wide,) + x.shape), blocks.reshape(wide)


def tiles_by_lag(retarded_tiles, tile_lags, column_of_block, block_of_slot, lags_wanted):
    columns = jnp.take(column_of_block, block_of_slot, axis=0)
    tiles = jnp.take(retarded_tiles[0], columns, axis=0)
    lags = jnp.take(tile_lags[0], columns, axis=0)
    zero = jnp.zeros_like(tiles[:, 0])
    return jnp.stack(
        [
            jnp.where(
                (lags[:, 0] == lag)[:, None, None],
                tiles[:, 0],
                jnp.where((lags[:, 1] == lag)[:, None, None], tiles[:, 1], zero),
            )
            for lag in lags_wanted
        ],
        axis=1,
    )


def rowwise(tiles, currents):
    spec = "slpq,slpr->qr" if tiles.ndim == 4 else "spq,spr->qr"
    return jnp.einsum(spec, tiles, currents, preferred_element_type=jnp.float32)


def per_device(wide, retarded_tiles, tile_lags, block_owner, later_current, excitation, inverse_blocks):
    lag_count = later_current.shape[0]
    step_count = excitation.shape[0]
    column_of_block = jnp.argsort(block_owner)

    split = (lag_count + 1) // 2
    bounds = [(0, split), (split, lag_count)] if lag_count > 1 else [(0, lag_count)]
    later = []
    for low, high in bounds:
        gathered, later_blocks = gather_blocks(later_current[low:high], wide, True)
        later.append((low, high, gathered))
    by_lag = tiles_by_lag(
        retarded_tiles, tile_lags, column_of_block, later_blocks, range(1, lag_count + 1)
    )
    inverse_t = inverse_blocks[0].T

    def advance(moment, retarded):
        source = excitation[moment] - retarded
        return jnp.dot(
            inverse_t, source, precision=lax.Precision.HIGHEST, preferred_element_type=jnp.float32
        )

    results = [None] * step_count
    newer = {}
    recent = None
    for moment in range(step_count - 1, -1, -1):
        first = max(1, step_count - moment)
        retarded = None
        for low, high, gathered in later:
            start = max(low, moment + first - step_count)
            stop = min(high, moment + lag_count + 1 - step_count)
            if start >= stop:
                continue
            term = rowwise(
                by_lag[:, start + step_count - moment - 1 : stop + step_count - moment - 1],
                gathered[:, start - low : stop - low],
            )
            retarded = term if retarded is None else retarded + term
        for delay in range(1, first):
            retarded = retarded + rowwise(recent[:, delay - 1], newer[moment + delay])
        current = advance(moment, retarded)
        results[moment] = current
        if moment > 0:
            newer[moment], new_blocks = gather_blocks(current.astype(jnp.bfloat16), wide, False)
            if recent is None:
                recent = tiles_by_lag(
                    retarded_tiles,
                    tile_lags,
                    column_of_block,
                    new_blocks,
                    range(1, min(lag_count, step_count - 1) + 1),
                )
    return jnp.stack(results)


def solution(mesh):
    in_specs = (
        P(("groups", "wide"), None, None, None, None),
        P(("groups", "wide"), None, None),
        P("groups"),
        P(None, ("groups", "wide"), None),
        P(None, ("groups", "wide"), None),
        P(("groups", "wide"), None, None),
    )
    out_specs = P(None, ("groups", "wide"), None)
    return jax.shard_map(
        functools.partial(per_device, mesh.shape["wide"]),
        mesh=mesh,
        in_specs=in_specs,
        out_specs=out_specs,
        check_vma=False,
    )
```

```python
import functools

import jax
import jax.numpy as jnp
import numpy as np
from jax import lax
from jax.sharding import PartitionSpec as P


def inner_size(wide):
    for size in (4, 2):
        if wide % size == 0:
            return size
    return 1


def line_stage(x, wide, inner):
    lines = wide // inner
    if lines <= 4:
        parts = [x]
        for shift in range(1, lines):
            pairs = [
                (d, ((d // inner + shift) % lines) * inner + d % inner) for d in range(wide)
            ]
            parts.append(lax.ppermute(x, "wide", pairs))
        return jnp.stack(parts), True
    groups = [[z * inner + k for z in range(lines)] for k in range(inner)]
    return lax.all_gather(x, "wide", axis=0, tiled=False, axis_index_groups=groups), False


def slab_stage(stack, wide, inner, doubling):
    if doubling and inner == 4:
        across = lax.ppermute(stack, "wide", [(d, d ^ 2) for d in range(wide)])
        beside = lax.ppermute(stack, "wide", [(d, d ^ 1) for d in range(wide)])
        diagonal = lax.ppermute(across, "wide", [(d, d ^ 1) for d in range(wide)])
        return jnp.stack([stack, beside, across, diagonal]), np.array([0, 1, 2, 3], np.int32)
    parts = [stack]
    for m in range(1, inner):
        parts.append(lax.ppermute(stack, "wide", [(d, d ^ m) for d in range(wide)]))
    return jnp.stack(parts), np.arange(inner, dtype=np.int32)


def gather_blocks(x, wide, doubling):
    inner = inner_size(wide)
    lines = wide // inner
    stack, shifted = line_stage(x, wide, inner)
    stack, masks = slab_stage(stack, wide, inner, doubling)
    me = lax.axis_index("wide")
    line = np.arange(lines, dtype=np.int32)
    source_line = (me // inner - line) % lines if shifted else jnp.asarray(line)
    blocks = (
        source_line[None, :] * inner
        + jnp.bitwise_xor(me % inner, jnp.asarray(masks))[:, None]
    )
    return stack.reshape((wide,) + x.shape), blocks.reshape(wide)


def tiles_by_lag(retarded_tiles, tile_lags, column_of_block, block_of_slot, lags_wanted):
    columns = jnp.take(column_of_block, block_of_slot, axis=0)
    tiles = jnp.take(retarded_tiles[0], columns, axis=0)
    lags = jnp.take(tile_lags[0], columns, axis=0)
    zero = jnp.zeros_like(tiles[:, 0])
    return jnp.stack(
        [
            jnp.where(
                (lags[:, 0] == lag)[:, None, None],
                tiles[:, 0],
                jnp.where((lags[:, 1] == lag)[:, None, None], tiles[:, 1], zero),
            )
            for lag in lags_wanted
        ],
        axis=1,
    )


def rowwise(tiles, currents):
    spec = "slpq,slpr->qr" if tiles.ndim == 4 else "spq,spr->qr"
    return jnp.einsum(spec, tiles, currents, preferred_element_type=jnp.float32)


def per_device(wide, retarded_tiles, tile_lags, block_owner, later_current, excitation, inverse_blocks):
    lag_count = later_current.shape[0]
    step_count = excitation.shape[0]
    column_of_block = jnp.argsort(block_owner)

    later, later_blocks = gather_blocks(later_current, wide, True)
    by_lag = tiles_by_lag(
        retarded_tiles, tile_lags, column_of_block, later_blocks, range(1, lag_count + 1)
    )
    inverse_t = inverse_blocks[0].T

    def advance(moment, retarded):
        source = excitation[moment] - retarded
        return jnp.dot(
            inverse_t, source, precision=lax.Precision.HIGHEST, preferred_element_type=jnp.float32
        )

    results = [None] * step_count
    newer = {}
    recent = None
    for moment in range(step_count - 1, -1, -1):
        first = max(1, step_count - moment)
        retarded = rowwise(
            by_lag[:, first - 1 :],
            later[:, moment + first - step_count : moment + lag_count + 1 - step_count],
        )
        for delay in range(1, first):
            retarded = retarded + rowwise(recent[:, delay - 1], newer[moment + delay])
        current = advance(moment, retarded)
        results[moment] = current
        if moment > 0:
            newer[moment], new_blocks = gather_blocks(current.astype(jnp.bfloat16), wide, False)
            if recent is None:
                recent = tiles_by_lag(
                    retarded_tiles,
                    tile_lags,
                    column_of_block,
                    new_blocks,
                    range(1, min(lag_count, step_count - 1) + 1),
                )
    return jnp.stack(results)


def solution(mesh):
    in_specs = (
        P(("groups", "wide"), None, None, None, None),
        P(("groups", "wide"), None, None),
        P("groups"),
        P(None, ("groups", "wide"), None),
        P(None, ("groups", "wide"), None),
        P(("groups", "wide"), None, None),
    )
    out_specs = P(None, ("groups", "wide"), None)
    return jax.shard_map(
        functools.partial(per_device, mesh.shape["wide"]),
        mesh=mesh,
        in_specs=in_specs,
        out_specs=out_specs,
        check_vma=False,
    )
```

```python
import functools

import jax
import jax.numpy as jnp
import numpy as np
from jax import lax
from jax.sharding import PartitionSpec as P


def inner_size(wide):
    for size in (4, 2):
        if wide % size == 0:
            return size
    return 1


def line_stage(x, wide, inner):
    lines = wide // inner
    if lines <= 4:
        parts = [x]
        for shift in range(1, lines):
            pairs = [
                (d, ((d // inner + shift) % lines) * inner + d % inner) for d in range(wide)
            ]
            parts.append(lax.ppermute(x, "wide", pairs))
        return jnp.stack(parts), True
    groups = [[z * inner + k for z in range(lines)] for k in range(inner)]
    return lax.all_gather(x, "wide", axis=0, tiled=False, axis_index_groups=groups), False


def slab_stage(stack, wide, inner, doubling):
    if doubling and inner == 4:
        across = lax.ppermute(stack, "wide", [(d, d ^ 2) for d in range(wide)])
        beside = lax.ppermute(stack, "wide", [(d, d ^ 1) for d in range(wide)])
        diagonal = lax.ppermute(across, "wide", [(d, d ^ 1) for d in range(wide)])
        return [stack, beside, across, diagonal]
    parts = [stack]
    for m in range(1, inner):
        parts.append(lax.ppermute(stack, "wide", [(d, d ^ m) for d in range(wide)]))
    return parts


def gather_blocks(x, wide, doubling):
    inner = inner_size(wide)
    lines = wide // inner
    stack, shifted = line_stage(x, wide, inner)
    pieces = slab_stage(stack, wide, inner, doubling)
    me = lax.axis_index("wide")
    line = np.arange(lines, dtype=np.int32)
    source_line = (me // inner - line) % lines if shifted else jnp.asarray(line)
    masks = np.arange(inner, dtype=np.int32)
    blocks = (
        source_line[None, :] * inner
        + jnp.bitwise_xor(me % inner, jnp.asarray(masks))[:, None]
    )
    return pieces, blocks.reshape(wide)


def tiles_by_lag(retarded_tiles, tile_lags, column_of_block, block_of_slot, lags_wanted):
    columns = jnp.take(column_of_block, block_of_slot, axis=0)
    tiles = jnp.take(retarded_tiles[0], columns, axis=0)
    lags = jnp.take(tile_lags[0], columns, axis=0)
    zero = jnp.zeros_like(tiles[:, 0])
    return jnp.stack(
        [
            jnp.where(
                (lags[:, 0] == lag)[:, None, None],
                tiles[:, 0],
                jnp.where((lags[:, 1] == lag)[:, None, None], tiles[:, 1], zero),
            )
            for lag in lags_wanted
        ],
        axis=1,
    )


def rowwise(tiles, currents):
    spec = "slpq,slpr->qr" if tiles.ndim == 4 else "spq,spr->qr"
    return jnp.einsum(spec, tiles, currents, preferred_element_type=jnp.float32)


def per_device(wide, retarded_tiles, tile_lags, block_owner, later_current, excitation, inverse_blocks):
    lag_count = later_current.shape[0]
    step_count = excitation.shape[0]
    column_of_block = jnp.argsort(block_owner)

    later, later_blocks = gather_blocks(later_current, wide, True)
    lines = later[0].shape[0]
    by_lag = tiles_by_lag(
        retarded_tiles, tile_lags, column_of_block, later_blocks, range(1, lag_count + 1)
    )
    inverse_t = inverse_blocks[0].T

    def advance(moment, retarded):
        source = excitation[moment] - retarded
        return jnp.dot(
            inverse_t, source, precision=lax.Precision.HIGHEST, preferred_element_type=jnp.float32
        )

    results = [None] * step_count
    newer = {}
    recent = None
    for moment in range(step_count - 1, -1, -1):
        first = max(1, step_count - moment)
        retarded = None
        for m, piece in enumerate(later):
            term = rowwise(
                by_lag[m * lines : (m + 1) * lines, first - 1 :],
                piece[:, moment + first - step_count : moment + lag_count + 1 - step_count],
            )
            retarded = term if retarded is None else retarded + term
        for delay in range(1, first):
            retarded = retarded + rowwise(recent[:, delay - 1], newer[moment + delay])
        current = advance(moment, retarded)
        results[moment] = current
        if moment > 0:
            pieces, new_blocks = gather_blocks(current.astype(jnp.bfloat16), wide, False)
            newer[moment] = jnp.concatenate(pieces)
            if recent is None:
                recent = tiles_by_lag(
                    retarded_tiles,
                    tile_lags,
                    column_of_block,
                    new_blocks,
                    range(1, min(lag_count, step_count - 1) + 1),
                )
    return jnp.stack(results)


def solution(mesh):
    in_specs = (
        P(("groups", "wide"), None, None, None, None),
        P(("groups", "wide"), None, None),
        P("groups"),
        P(None, ("groups", "wide"), None),
        P(None, ("groups", "wide"), None),
        P(("groups", "wide"), None, None),
    )
    out_specs = P(None, ("groups", "wide"), None)
    return jax.shard_map(
        functools.partial(per_device, mesh.shape["wide"]),
        mesh=mesh,
        in_specs=in_specs,
        out_specs=out_specs,
        check_vma=False,
    )
```

```python
import functools

import jax
import jax.numpy as jnp
import numpy as np
from jax import lax
from jax.sharding import PartitionSpec as P


def inner_size(wide):
    for size in (4, 2):
        if wide % size == 0:
            return size
    return 1


def line_stage(x, wide, inner):
    lines = wide // inner
    if lines <= 4:
        parts = [x[None]]
        for shift in range(1, lines):
            pairs = [
                (d, ((d // inner + shift) % lines) * inner + d % inner) for d in range(wide)
            ]
            parts.append(lax.ppermute(x, "wide", pairs)[None])
        return parts, True
    groups = [[z * inner + k for z in range(lines)] for k in range(inner)]
    return [lax.all_gather(x, "wide", axis=0, tiled=False, axis_index_groups=groups)], False


def swap(x, wide, mask):
    return lax.ppermute(x, "wide", [(d, d ^ mask) for d in range(wide)])


def gather_blocks(x, wide, early):
    inner = inner_size(wide)
    lines = wide // inner
    parts, shifted = line_stage(x, wide, inner)
    own = parts[0] if len(parts) == 1 else jnp.concatenate(parts)
    every = list(range(lines))
    pieces = [(own, 0, every)]
    if early and inner == 4 and len(parts) > 1:
        rest = jnp.concatenate(parts[1:])
        across_own = swap(parts[0], wide, 2)
        across_rest = swap(rest, wide, 2)
        pieces += [
            (swap(own, wide, 1), 1, every),
            (across_own, 2, every[:1]),
            (across_rest, 2, every[1:]),
            (swap(across_own, wide, 1), 3, every[:1]),
            (swap(across_rest, wide, 1), 3, every[1:]),
        ]
    else:
        pieces += [(swap(own, wide, m), m, every) for m in range(1, inner)]
    me = lax.axis_index("wide")
    line = np.arange(lines, dtype=np.int32)
    source_line = (me // inner - line) % lines if shifted else jnp.asarray(line)
    blocks = jnp.concatenate(
        [source_line[np.array(held)] * inner + jnp.bitwise_xor(me % inner, m) for _, m, held in pieces]
    )
    return [piece for piece, _, _ in pieces], blocks


def tiles_by_lag(retarded_tiles, tile_lags, column_of_block, block_of_slot, lags_wanted):
    columns = jnp.take(column_of_block, block_of_slot, axis=0)
    tiles = jnp.take(retarded_tiles[0], columns, axis=0)
    lags = jnp.take(tile_lags[0], columns, axis=0)
    zero = jnp.zeros_like(tiles[:, 0])
    return jnp.stack(
        [
            jnp.where(
                (lags[:, 0] == lag)[:, None, None],
                tiles[:, 0],
                jnp.where((lags[:, 1] == lag)[:, None, None], tiles[:, 1], zero),
            )
            for lag in lags_wanted
        ],
        axis=1,
    )


def rowwise(tiles, currents):
    spec = "slpq,slpr->qr" if tiles.ndim == 4 else "spq,spr->qr"
    return jnp.einsum(spec, tiles, currents, preferred_element_type=jnp.float32)


def per_device(wide, retarded_tiles, tile_lags, block_owner, later_current, excitation, inverse_blocks):
    lag_count = later_current.shape[0]
    step_count = excitation.shape[0]
    column_of_block = jnp.argsort(block_owner)

    later, later_blocks = gather_blocks(later_current, wide, True)
    offsets = np.cumsum([0] + [piece.shape[0] for piece in later])
    by_lag = tiles_by_lag(
        retarded_tiles, tile_lags, column_of_block, later_blocks, range(1, lag_count + 1)
    )
    inverse_t = inverse_blocks[0].T

    def advance(moment, retarded):
        source = excitation[moment] - retarded
        return jnp.dot(
            inverse_t, source, precision=lax.Precision.HIGHEST, preferred_element_type=jnp.float32
        )

    results = [None] * step_count
    newer = {}
    recent = None
    for moment in range(step_count - 1, -1, -1):
        first = max(1, step_count - moment)
        retarded = None
        for m, piece in enumerate(later):
            term = rowwise(
                by_lag[offsets[m] : offsets[m + 1], first - 1 :],
                piece[:, moment + first - step_count : moment + lag_count + 1 - step_count],
            )
            retarded = term if retarded is None else retarded + term
        for delay in range(1, first):
            retarded = retarded + rowwise(recent[:, delay - 1], newer[moment + delay])
        current = advance(moment, retarded)
        results[moment] = current
        if moment > 0:
            pieces, new_blocks = gather_blocks(current.astype(jnp.bfloat16), wide, False)
            newer[moment] = jnp.concatenate(pieces)
            if recent is None:
                recent = tiles_by_lag(
                    retarded_tiles,
                    tile_lags,
                    column_of_block,
                    new_blocks,
                    range(1, min(lag_count, step_count - 1) + 1),
                )
    return jnp.stack(results)


def solution(mesh):
    in_specs = (
        P(("groups", "wide"), None, None, None, None),
        P(("groups", "wide"), None, None),
        P("groups"),
        P(None, ("groups", "wide"), None),
        P(None, ("groups", "wide"), None),
        P(("groups", "wide"), None, None),
    )
    out_specs = P(None, ("groups", "wide"), None)
    return jax.shard_map(
        functools.partial(per_device, mesh.shape["wide"]),
        mesh=mesh,
        in_specs=in_specs,
        out_specs=out_specs,
        check_vma=False,
    )
```

```python
import functools

import jax
import jax.numpy as jnp
import numpy as np
from jax import lax
from jax.sharding import PartitionSpec as P


def inner_size(wide):
    for size in (4, 2):
        if wide % size == 0:
            return size
    return 1


def line_stage(x, wide, inner):
    lines = wide // inner
    if lines <= 4:
        parts = [x]
        for shift in range(1, lines):
            pairs = [
                (d, ((d // inner + shift) % lines) * inner + d % inner) for d in range(wide)
            ]
            parts.append(lax.ppermute(x, "wide", pairs))
        return jnp.stack(parts), True
    groups = [[z * inner + k for z in range(lines)] for k in range(inner)]
    return lax.all_gather(x, "wide", axis=0, tiled=False, axis_index_groups=groups), False


def slab_stage(stack, wide, inner, doubling):
    if doubling and inner == 4:
        across = lax.ppermute(stack, "wide", [(d, d ^ 2) for d in range(wide)])
        beside = lax.ppermute(stack, "wide", [(d, d ^ 1) for d in range(wide)])
        diagonal = lax.ppermute(across, "wide", [(d, d ^ 1) for d in range(wide)])
        return [stack, beside, across, diagonal]
    if inner == 4:
        slabs = [[z * inner + k for k in range(inner)] for z in range(wide // inner)]
        gathered = lax.all_gather(stack, "wide", axis=0, tiled=False, axis_index_groups=slabs)
        return [gathered[k] for k in range(inner)]
    parts = [stack]
    for m in range(1, inner):
        parts.append(lax.ppermute(stack, "wide", [(d, d ^ m) for d in range(wide)]))
    return parts


def gather_blocks(x, wide, doubling):
    inner = inner_size(wide)
    lines = wide // inner
    stack, shifted = line_stage(x, wide, inner)
    pieces = slab_stage(stack, wide, inner, doubling)
    me = lax.axis_index("wide")
    line = np.arange(lines, dtype=np.int32)
    source_line = (me // inner - line) % lines if shifted else jnp.asarray(line)
    masks = np.arange(inner, dtype=np.int32)
    position = jnp.asarray(masks) if not doubling and inner == 4 else jnp.bitwise_xor(me % inner, jnp.asarray(masks))
    blocks = source_line[None, :] * inner + position[:, None]
    return pieces, blocks.reshape(wide)


def tiles_by_lag(retarded_tiles, tile_lags, column_of_block, block_of_slot, lags_wanted):
    columns = jnp.take(column_of_block, block_of_slot, axis=0)
    tiles = jnp.take(retarded_tiles[0], columns, axis=0)
    lags = jnp.take(tile_lags[0], columns, axis=0)
    zero = jnp.zeros_like(tiles[:, 0])
    return jnp.stack(
        [
            jnp.where(
                (lags[:, 0] == lag)[:, None, None],
                tiles[:, 0],
                jnp.where((lags[:, 1] == lag)[:, None, None], tiles[:, 1], zero),
            )
            for lag in lags_wanted
        ],
        axis=1,
    )


def rowwise(tiles, currents):
    spec = "slpq,slpr->qr" if tiles.ndim == 4 else "spq,spr->qr"
    return jnp.einsum(spec, tiles, currents, preferred_element_type=jnp.float32)


def per_device(wide, retarded_tiles, tile_lags, block_owner, later_current, excitation, inverse_blocks):
    lag_count = later_current.shape[0]
    step_count = excitation.shape[0]
    column_of_block = jnp.argsort(block_owner)

    later, later_blocks = gather_blocks(later_current, wide, True)
    lines = later[0].shape[0]
    by_lag = tiles_by_lag(
        retarded_tiles, tile_lags, column_of_block, later_blocks, range(1, lag_count + 1)
    )
    inverse_t = inverse_blocks[0].T

    def advance(moment, retarded):
        source = excitation[moment] - retarded
        return jnp.dot(
            inverse_t, source, precision=lax.Precision.HIGHEST, preferred_element_type=jnp.float32
        )

    results = [None] * step_count
    newer = {}
    recent = None
    for moment in range(step_count - 1, -1, -1):
        first = max(1, step_count - moment)
        retarded = None
        for m, piece in enumerate(later):
            term = rowwise(
                by_lag[m * lines : (m + 1) * lines, first - 1 :],
                piece[:, moment + first - step_count : moment + lag_count + 1 - step_count],
            )
            retarded = term if retarded is None else retarded + term
        for delay in range(1, first):
            retarded = retarded + rowwise(recent[:, delay - 1], newer[moment + delay])
        current = advance(moment, retarded)
        results[moment] = current
        if moment > 0:
            pieces, new_blocks = gather_blocks(current.astype(jnp.bfloat16), wide, False)
            newer[moment] = jnp.concatenate(pieces)
            if recent is None:
                recent = tiles_by_lag(
                    retarded_tiles,
                    tile_lags,
                    column_of_block,
                    new_blocks,
                    range(1, min(lag_count, step_count - 1) + 1),
                )
    return jnp.stack(results)


def solution(mesh):
    in_specs = (
        P(("groups", "wide"), None, None, None, None),
        P(("groups", "wide"), None, None),
        P("groups"),
        P(None, ("groups", "wide"), None),
        P(None, ("groups", "wide"), None),
        P(("groups", "wide"), None, None),
    )
    out_specs = P(None, ("groups", "wide"), None)
    return jax.shard_map(
        functools.partial(per_device, mesh.shape["wide"]),
        mesh=mesh,
        in_specs=in_specs,
        out_specs=out_specs,
        check_vma=False,
    )
```

```python
import functools

import jax
import jax.numpy as jnp
import numpy as np
from jax import lax
from jax.sharding import PartitionSpec as P


def inner_size(wide):
    for size in (4, 2):
        if wide % size == 0:
            return size
    return 1


def line_stage(x, wide, inner):
    lines = wide // inner
    if lines <= 4:
        parts = [x]
        for shift in range(1, lines):
            pairs = [
                (d, ((d // inner + shift) % lines) * inner + d % inner) for d in range(wide)
            ]
            parts.append(lax.ppermute(x, "wide", pairs))
        return jnp.stack(parts), True
    groups = [[z * inner + k for z in range(lines)] for k in range(inner)]
    return lax.all_gather(x, "wide", axis=0, tiled=False, axis_index_groups=groups), False


def slab_stage(stack, wide, inner, doubling):
    if doubling and inner == 4:
        across = lax.ppermute(stack, "wide", [(d, d ^ 2) for d in range(wide)])
        beside = lax.ppermute(stack, "wide", [(d, d ^ 1) for d in range(wide)])
        diagonal = lax.ppermute(across, "wide", [(d, d ^ 1) for d in range(wide)])
        return [stack, beside, across, diagonal]
    parts = [stack]
    for m in range(1, inner):
        parts.append(lax.ppermute(stack, "wide", [(d, d ^ m) for d in range(wide)]))
    return parts


def gather_blocks(x, wide, doubling):
    inner = inner_size(wide)
    lines = wide // inner
    stack, shifted = line_stage(x, wide, inner)
    pieces = slab_stage(stack, wide, inner, doubling)
    me = lax.axis_index("wide")
    line = np.arange(lines, dtype=np.int32)
    source_line = (me // inner - line) % lines if shifted else jnp.asarray(line)
    masks = np.arange(inner, dtype=np.int32)
    blocks = (
        source_line[None, :] * inner
        + jnp.bitwise_xor(me % inner, jnp.asarray(masks))[:, None]
    )
    return pieces, blocks.reshape(wide)


def tiles_by_lag(retarded_tiles, tile_lags, column_of_block, block_of_slot, lags_wanted):
    columns = jnp.take(column_of_block, block_of_slot, axis=0)
    tiles = jnp.take(retarded_tiles[0], columns, axis=0)
    lags = jnp.take(tile_lags[0], columns, axis=0)
    zero = jnp.zeros_like(tiles[:, 0])
    return jnp.stack(
        [
            jnp.where(
                (lags[:, 0] == lag)[:, None, None],
                tiles[:, 0],
                jnp.where((lags[:, 1] == lag)[:, None, None], tiles[:, 1], zero),
            )
            for lag in lags_wanted
        ],
        axis=1,
    )


def rowwise(tiles, currents):
    spec = "slpq,slpr->qr" if tiles.ndim == 4 else "spq,spr->qr"
    return jnp.einsum(spec, tiles, currents, preferred_element_type=jnp.float32)


def per_device(wide, retarded_tiles, tile_lags, block_owner, later_current, excitation, inverse_blocks):
    lag_count = later_current.shape[0]
    step_count = excitation.shape[0]
    column_of_block = jnp.argsort(block_owner)

    later, later_blocks = gather_blocks(later_current, wide, True)
    lines = later[0].shape[0]
    by_lag = tiles_by_lag(
        retarded_tiles, tile_lags, column_of_block, later_blocks, range(1, lag_count + 1)
    )
    inverse_t = inverse_blocks[0].T

    def advance(moment, retarded):
        source = excitation[moment] - retarded
        return jnp.dot(
            inverse_t, source, precision=lax.Precision.HIGHEST, preferred_element_type=jnp.float32
        )

    results = [None] * step_count
    newer = {}
    recent = None
    for moment in range(step_count - 1, -1, -1):
        first = max(1, step_count - moment)
        retarded = None
        for m, piece in enumerate(later):
            term = rowwise(
                by_lag[m * lines : (m + 1) * lines, first - 1 :],
                piece[:, moment + first - step_count : moment + lag_count + 1 - step_count],
            )
            retarded = term if retarded is None else retarded + term
        for delay in range(1, first):
            retarded = retarded + rowwise(recent[:, delay - 1], newer[moment + delay])
        current = advance(moment, retarded)
        results[moment] = current
        if moment > 0:
            pieces, new_blocks = gather_blocks(current.astype(jnp.bfloat16), wide, True)
            newer[moment] = jnp.concatenate(pieces)
            if recent is None:
                recent = tiles_by_lag(
                    retarded_tiles,
                    tile_lags,
                    column_of_block,
                    new_blocks,
                    range(1, min(lag_count, step_count - 1) + 1),
                )
    return jnp.stack(results)


def solution(mesh):
    in_specs = (
        P(("groups", "wide"), None, None, None, None),
        P(("groups", "wide"), None, None),
        P("groups"),
        P(None, ("groups", "wide"), None),
        P(None, ("groups", "wide"), None),
        P(("groups", "wide"), None, None),
    )
    out_specs = P(None, ("groups", "wide"), None)
    return jax.shard_map(
        functools.partial(per_device, mesh.shape["wide"]),
        mesh=mesh,
        in_specs=in_specs,
        out_specs=out_specs,
        check_vma=False,
    )
```

```python
import functools

import jax
import jax.numpy as jnp
import numpy as np
from jax import lax
from jax.sharding import PartitionSpec as P


def inner_size(wide):
    for size in (4, 2):
        if wide % size == 0:
            return size
    return 1


def line_stage(x, wide, inner):
    lines = wide // inner
    if lines <= 4:
        parts = [x[None]]
        for shift in range(1, lines):
            pairs = [
                (d, ((d // inner + shift) % lines) * inner + d % inner) for d in range(wide)
            ]
            parts.append(lax.ppermute(x, "wide", pairs)[None])
        return parts, True
    groups = [[z * inner + k for z in range(lines)] for k in range(inner)]
    return [lax.all_gather(x, "wide", axis=0, tiled=False, axis_index_groups=groups)], False


def swap(x, wide, mask):
    return lax.ppermute(x, "wide", [(d, d ^ mask) for d in range(wide)])


def slab_stage(parts, wide, inner, early):
    stack = parts[0] if len(parts) == 1 else jnp.concatenate(parts)
    if inner != 4:
        return [stack] + [swap(stack, wide, m) for m in range(1, inner)]
    if early and len(parts) > 1:
        rest = jnp.concatenate(parts[1:])
        across_own = swap(parts[0], wide, 2)
        across_rest = swap(rest, wide, 2)
        return [
            stack,
            swap(stack, wide, 1),
            across_own,
            across_rest,
            swap(across_own, wide, 1),
            swap(across_rest, wide, 1),
        ]
    across = swap(stack, wide, 2)
    return [stack, swap(stack, wide, 1), across, swap(across, wide, 1)]


def gather_blocks(x, wide, early):
    inner = inner_size(wide)
    lines = wide // inner
    parts, shifted = line_stage(x, wide, inner)
    pieces = slab_stage(parts, wide, inner, early)
    me = lax.axis_index("wide")
    line = np.arange(lines, dtype=np.int32)
    source_line = (me // inner - line) % lines if shifted else jnp.asarray(line)
    masks = np.arange(inner, dtype=np.int32)
    blocks = (
        source_line[None, :] * inner
        + jnp.bitwise_xor(me % inner, jnp.asarray(masks))[:, None]
    )
    return pieces, blocks.reshape(wide)


def tiles_by_lag(retarded_tiles, tile_lags, column_of_block, block_of_slot, lags_wanted):
    columns = jnp.take(column_of_block, block_of_slot, axis=0)
    tiles = jnp.take(retarded_tiles[0], columns, axis=0)
    lags = jnp.take(tile_lags[0], columns, axis=0)
    zero = jnp.zeros_like(tiles[:, 0])
    return jnp.stack(
        [
            jnp.where(
                (lags[:, 0] == lag)[:, None, None],
                tiles[:, 0],
                jnp.where((lags[:, 1] == lag)[:, None, None], tiles[:, 1], zero),
            )
            for lag in lags_wanted
        ],
        axis=1,
    )


def rowwise(tiles, currents):
    spec = "slpq,slpr->qr" if tiles.ndim == 4 else "spq,spr->qr"
    return jnp.einsum(spec, tiles, currents, preferred_element_type=jnp.float32)


def per_device(wide, retarded_tiles, tile_lags, block_owner, later_current, excitation, inverse_blocks):
    lag_count = later_current.shape[0]
    step_count = excitation.shape[0]
    column_of_block = jnp.argsort(block_owner)

    later, later_blocks = gather_blocks(later_current, wide, True)
    offsets = np.cumsum([0] + [piece.shape[0] for piece in later])
    by_lag = tiles_by_lag(
        retarded_tiles, tile_lags, column_of_block, later_blocks, range(1, lag_count + 1)
    )
    inverse_t = inverse_blocks[0].T

    def advance(moment, retarded):
        source = excitation[moment] - retarded
        return jnp.dot(
            inverse_t, source, precision=lax.Precision.HIGHEST, preferred_element_type=jnp.float32
        )

    results = [None] * step_count
    newer = {}
    recent = None
    for moment in range(step_count - 1, -1, -1):
        first = max(1, step_count - moment)
        retarded = None
        for m, piece in enumerate(later):
            term = rowwise(
                by_lag[offsets[m] : offsets[m + 1], first - 1 :],
                piece[:, moment + first - step_count : moment + lag_count + 1 - step_count],
            )
            retarded = term if retarded is None else retarded + term
        for delay in range(1, first):
            retarded = retarded + rowwise(recent[:, delay - 1], newer[moment + delay])
        current = advance(moment, retarded)
        results[moment] = current
        if moment > 0:
            pieces, new_blocks = gather_blocks(current.astype(jnp.bfloat16), wide, False)
            newer[moment] = jnp.concatenate(pieces)
            if recent is None:
                recent = tiles_by_lag(
                    retarded_tiles,
                    tile_lags,
                    column_of_block,
                    new_blocks,
                    range(1, min(lag_count, step_count - 1) + 1),
                )
    return jnp.stack(results)


def solution(mesh):
    in_specs = (
        P(("groups", "wide"), None, None, None, None),
        P(("groups", "wide"), None, None),
        P("groups"),
        P(None, ("groups", "wide"), None),
        P(None, ("groups", "wide"), None),
        P(("groups", "wide"), None, None),
    )
    out_specs = P(None, ("groups", "wide"), None)
    return jax.shard_map(
        functools.partial(per_device, mesh.shape["wide"]),
        mesh=mesh,
        in_specs=in_specs,
        out_specs=out_specs,
        check_vma=False,
    )
```

```python
import functools

import jax
import jax.numpy as jnp
import numpy as np
from jax import lax
from jax.sharding import PartitionSpec as P


def inner_size(wide):
    for size in (4, 2):
        if wide % size == 0:
            return size
    return 1


def line_stage(x, wide, inner):
    lines = wide // inner
    if lines <= 4:
        parts = [x[None]]
        for shift in range(1, lines):
            pairs = [
                (d, ((d // inner + shift) % lines) * inner + d % inner) for d in range(wide)
            ]
            parts.append(lax.ppermute(x, "wide", pairs)[None])
        return parts, True
    groups = [[z * inner + k for z in range(lines)] for k in range(inner)]
    return [lax.all_gather(x, "wide", axis=0, tiled=False, axis_index_groups=groups)], False


def swap(x, wide, mask):
    return lax.ppermute(x, "wide", [(d, d ^ mask) for d in range(wide)])


def slab_stage(parts, wide, inner, early):
    stack = parts[0] if len(parts) == 1 else jnp.concatenate(parts)
    if inner != 4:
        return [stack] + [swap(stack, wide, m) for m in range(1, inner)]
    if early and len(parts) > 1:
        rest = jnp.concatenate(parts[1:])
        across_own = swap(parts[0], wide, 2)
        across_rest = swap(rest, wide, 2)
        return [
            stack,
            swap(stack, wide, 1),
            across_own,
            across_rest,
            swap(across_own, wide, 1),
            swap(across_rest, wide, 1),
        ]
    across = swap(stack, wide, 2)
    return [stack, swap(stack, wide, 1), across, swap(across, wide, 1)]


def gather_blocks(x, wide, early):
    inner = inner_size(wide)
    lines = wide // inner
    parts, shifted = line_stage(x, wide, inner)
    pieces = slab_stage(parts, wide, inner, early)
    me = lax.axis_index("wide")
    line = np.arange(lines, dtype=np.int32)
    source_line = (me // inner - line) % lines if shifted else jnp.asarray(line)
    masks = np.arange(inner, dtype=np.int32)
    blocks = (
        source_line[None, :] * inner
        + jnp.bitwise_xor(me % inner, jnp.asarray(masks))[:, None]
    )
    return pieces, blocks.reshape(wide)


def tiles_by_lag(retarded_tiles, tile_lags, column_of_block, block_of_slot, lags_wanted):
    columns = jnp.take(column_of_block, block_of_slot, axis=0)
    tiles = jnp.take(retarded_tiles[0], columns, axis=0)
    lags = jnp.take(tile_lags[0], columns, axis=0)
    zero = jnp.zeros_like(tiles[:, 0])
    return jnp.stack(
        [
            jnp.where(
                (lags[:, 0] == lag)[:, None, None],
                tiles[:, 0],
                jnp.where((lags[:, 1] == lag)[:, None, None], tiles[:, 1], zero),
            )
            for lag in lags_wanted
        ],
        axis=1,
    )


def rowwise(tiles, currents):
    spec = "slpq,slpr->qr" if tiles.ndim == 4 else "spq,spr->qr"
    return jnp.einsum(spec, tiles, currents, preferred_element_type=jnp.float32)


def per_device(wide, retarded_tiles, tile_lags, block_owner, later_current, excitation, inverse_blocks):
    lag_count = later_current.shape[0]
    step_count = excitation.shape[0]
    column_of_block = jnp.argsort(block_owner)

    later, later_blocks = gather_blocks(later_current, wide, True)
    offsets = np.cumsum([0] + [piece.shape[0] for piece in later])
    by_lag = tiles_by_lag(
        retarded_tiles, tile_lags, column_of_block, later_blocks, range(1, lag_count + 1)
    )
    inverse_t = inverse_blocks[0].T

    def advance(moment, retarded):
        source = excitation[moment] - retarded
        return jnp.dot(
            inverse_t, source, precision=lax.Precision.HIGHEST, preferred_element_type=jnp.float32
        )

    results = [None] * step_count
    newer = {}
    recent = None
    for moment in range(step_count - 1, -1, -1):
        first = max(1, step_count - moment)
        retarded = None
        for m, piece in enumerate(later):
            term = rowwise(
                by_lag[offsets[m] : offsets[m + 1], first - 1 :],
                piece[:, moment + first - step_count : moment + lag_count + 1 - step_count],
            )
            retarded = term if retarded is None else retarded + term
        for delay in range(1, first):
            retarded = retarded + rowwise(recent[:, delay - 1], newer[moment + delay])
        current = advance(moment, retarded)
        results[moment] = current
        if moment > 0:
            pieces, new_blocks = gather_blocks(current.astype(jnp.bfloat16), wide, True)
            newer[moment] = jnp.concatenate(pieces)
            if recent is None:
                recent = tiles_by_lag(
                    retarded_tiles,
                    tile_lags,
                    column_of_block,
                    new_blocks,
                    range(1, min(lag_count, step_count - 1) + 1),
                )
    return jnp.stack(results)


def solution(mesh):
    in_specs = (
        P(("groups", "wide"), None, None, None, None),
        P(("groups", "wide"), None, None),
        P("groups"),
        P(None, ("groups", "wide"), None),
        P(None, ("groups", "wide"), None),
        P(("groups", "wide"), None, None),
    )
    out_specs = P(None, ("groups", "wide"), None)
    return jax.shard_map(
        functools.partial(per_device, mesh.shape["wide"]),
        mesh=mesh,
        in_specs=in_specs,
        out_specs=out_specs,
        check_vma=False,
    )
```

```python
import functools

import jax
import jax.numpy as jnp
import numpy as np
from jax import lax
from jax.sharding import PartitionSpec as P


def inner_size(wide):
    for size in (4, 2):
        if wide % size == 0:
            return size
    return 1


def line_stage(x, wide, inner):
    lines = wide // inner
    if lines <= 4:
        parts = [x[None]]
        for shift in range(1, lines):
            pairs = [
                (d, ((d // inner + shift) % lines) * inner + d % inner) for d in range(wide)
            ]
            parts.append(lax.ppermute(x, "wide", pairs)[None])
        return parts, True
    groups = [[z * inner + k for z in range(lines)] for k in range(inner)]
    return [lax.all_gather(x, "wide", axis=0, tiled=False, axis_index_groups=groups)], False


def swap(x, wide, mask):
    return lax.ppermute(x, "wide", [(d, d ^ mask) for d in range(wide)])


def slab_stage(parts, wide, inner, early, direct=False):
    stack = parts[0] if len(parts) == 1 else jnp.concatenate(parts)
    if inner != 4:
        return [stack] + [swap(stack, wide, m) for m in range(1, inner)]
    if early and len(parts) > 1:
        rest = jnp.concatenate(parts[1:])
        across_own = swap(parts[0], wide, 2)
        across_rest = swap(rest, wide, 2)
        diagonal_own = swap(parts[0], wide, 3) if direct else swap(across_own, wide, 1)
        diagonal_rest = swap(rest, wide, 3) if direct else swap(across_rest, wide, 1)
        return [stack, swap(stack, wide, 1), across_own, across_rest, diagonal_own, diagonal_rest]
    across = swap(stack, wide, 2)
    return [stack, swap(stack, wide, 1), across, swap(across, wide, 1)]


def gather_blocks(x, wide, early, direct=False):
    inner = inner_size(wide)
    lines = wide // inner
    parts, shifted = line_stage(x, wide, inner)
    pieces = slab_stage(parts, wide, inner, early, direct)
    me = lax.axis_index("wide")
    line = np.arange(lines, dtype=np.int32)
    source_line = (me // inner - line) % lines if shifted else jnp.asarray(line)
    masks = np.arange(inner, dtype=np.int32)
    blocks = (
        source_line[None, :] * inner
        + jnp.bitwise_xor(me % inner, jnp.asarray(masks))[:, None]
    )
    return pieces, blocks.reshape(wide)


def tiles_by_lag(retarded_tiles, tile_lags, column_of_block, block_of_slot, lags_wanted):
    columns = jnp.take(column_of_block, block_of_slot, axis=0)
    tiles = jnp.take(retarded_tiles[0], columns, axis=0)
    lags = jnp.take(tile_lags[0], columns, axis=0)
    zero = jnp.zeros_like(tiles[:, 0])
    return jnp.stack(
        [
            jnp.where(
                (lags[:, 0] == lag)[:, None, None],
                tiles[:, 0],
                jnp.where((lags[:, 1] == lag)[:, None, None], tiles[:, 1], zero),
            )
            for lag in lags_wanted
        ],
        axis=1,
    )


def rowwise(tiles, currents):
    spec = "slpq,slpr->qr" if tiles.ndim == 4 else "spq,spr->qr"
    return jnp.einsum(spec, tiles, currents, preferred_element_type=jnp.float32)


def per_device(wide, retarded_tiles, tile_lags, block_owner, later_current, excitation, inverse_blocks):
    lag_count = later_current.shape[0]
    step_count = excitation.shape[0]
    column_of_block = jnp.argsort(block_owner)

    later, later_blocks = gather_blocks(later_current, wide, True)
    offsets = np.cumsum([0] + [piece.shape[0] for piece in later])
    by_lag = tiles_by_lag(
        retarded_tiles, tile_lags, column_of_block, later_blocks, range(1, lag_count + 1)
    )
    inverse_t = inverse_blocks[0].T

    def advance(moment, retarded):
        source = excitation[moment] - retarded
        return jnp.dot(
            inverse_t, source, precision=lax.Precision.HIGHEST, preferred_element_type=jnp.float32
        )

    results = [None] * step_count
    newer = {}
    recent = None
    for moment in range(step_count - 1, -1, -1):
        first = max(1, step_count - moment)
        retarded = None
        for m, piece in enumerate(later):
            term = rowwise(
                by_lag[offsets[m] : offsets[m + 1], first - 1 :],
                piece[:, moment + first - step_count : moment + lag_count + 1 - step_count],
            )
            retarded = term if retarded is None else retarded + term
        for delay in range(1, first):
            retarded = retarded + rowwise(recent[:, delay - 1], newer[moment + delay])
        current = advance(moment, retarded)
        results[moment] = current
        if moment > 0:
            pieces, new_blocks = gather_blocks(current.astype(jnp.bfloat16), wide, True, direct=True)
            newer[moment] = jnp.concatenate(pieces)
            if recent is None:
                recent = tiles_by_lag(
                    retarded_tiles,
                    tile_lags,
                    column_of_block,
                    new_blocks,
                    range(1, min(lag_count, step_count - 1) + 1),
                )
    return jnp.stack(results)


def solution(mesh):
    in_specs = (
        P(("groups", "wide"), None, None, None, None),
        P(("groups", "wide"), None, None),
        P("groups"),
        P(None, ("groups", "wide"), None),
        P(None, ("groups", "wide"), None),
        P(("groups", "wide"), None, None),
    )
    out_specs = P(None, ("groups", "wide"), None)
    return jax.shard_map(
        functools.partial(per_device, mesh.shape["wide"]),
        mesh=mesh,
        in_specs=in_specs,
        out_specs=out_specs,
        check_vma=False,
    )
```

```python
import functools

import jax
import jax.numpy as jnp
import numpy as np
from jax import lax
from jax.sharding import PartitionSpec as P


def inner_size(wide):
    for size in (4, 2):
        if wide % size == 0:
            return size
    return 1


def line_stage(x, wide, inner):
    lines = wide // inner
    if lines <= 4:
        parts = [x[None]]
        for shift in range(1, lines):
            pairs = [
                (d, ((d // inner + shift) % lines) * inner + d % inner) for d in range(wide)
            ]
            parts.append(lax.ppermute(x, "wide", pairs)[None])
        return parts, True
    groups = [[z * inner + k for z in range(lines)] for k in range(inner)]
    return [lax.all_gather(x, "wide", axis=0, tiled=False, axis_index_groups=groups)], False


def swap(x, wide, mask):
    return lax.ppermute(x, "wide", [(d, d ^ mask) for d in range(wide)])


def slab_stage(parts, wide, inner, early):
    stack = parts[0] if len(parts) == 1 else jnp.concatenate(parts)
    if inner != 4:
        return [stack] + [swap(stack, wide, m) for m in range(1, inner)]
    if early and len(parts) > 1:
        rest = jnp.concatenate(parts[1:])
        across_own = swap(parts[0], wide, 2)
        across_rest = swap(rest, wide, 2)
        return [
            stack,
            swap(stack, wide, 1),
            across_own,
            across_rest,
            swap(across_own, wide, 1),
            swap(across_rest, wide, 1),
        ]
    across = swap(stack, wide, 2)
    return [stack, swap(stack, wide, 1), across, swap(across, wide, 1)]


def gather_blocks(x, wide, early):
    inner = inner_size(wide)
    lines = wide // inner
    parts, shifted = line_stage(x, wide, inner)
    pieces = slab_stage(parts, wide, inner, early)
    me = lax.axis_index("wide")
    line = np.arange(lines, dtype=np.int32)
    source_line = (me // inner - line) % lines if shifted else jnp.asarray(line)
    masks = np.arange(inner, dtype=np.int32)
    blocks = (
        source_line[None, :] * inner
        + jnp.bitwise_xor(me % inner, jnp.asarray(masks))[:, None]
    )
    return pieces, blocks.reshape(wide)


def tiles_by_lag(retarded_tiles, tile_lags, column_of_block, block_of_slot, lags_wanted):
    columns = jnp.take(column_of_block, block_of_slot, axis=0)
    tiles = jnp.take(retarded_tiles[0], columns, axis=0)
    lags = jnp.take(tile_lags[0], columns, axis=0)
    zero = jnp.zeros_like(tiles[:, 0])
    return jnp.stack(
        [
            jnp.where(
                (lags[:, 0] == lag)[:, None, None],
                tiles[:, 0],
                jnp.where((lags[:, 1] == lag)[:, None, None], tiles[:, 1], zero),
            )
            for lag in lags_wanted
        ],
        axis=1,
    )


def rowwise(tiles, currents):
    spec = "slpq,slpr->qr" if tiles.ndim == 4 else "spq,spr->qr"
    return jnp.einsum(spec, tiles, currents, preferred_element_type=jnp.float32)


def per_device(wide, retarded_tiles, tile_lags, block_owner, later_current, excitation, inverse_blocks):
    lag_count = later_current.shape[0]
    step_count = excitation.shape[0]
    column_of_block = jnp.argsort(block_owner)

    later, later_blocks = gather_blocks(later_current, wide, True)
    offsets = np.cumsum([0] + [piece.shape[0] for piece in later])
    by_lag = tiles_by_lag(
        retarded_tiles, tile_lags, column_of_block, later_blocks, range(1, lag_count + 1)
    )
    inverse_t = inverse_blocks[0].T

    def advance(moment, retarded):
        source = excitation[moment] - retarded
        return jnp.dot(
            inverse_t, source, precision=lax.Precision.HIGHEST, preferred_element_type=jnp.float32
        )

    results = [None] * step_count
    newer = {}
    recent = None
    for moment in range(step_count - 1, -1, -1):
        first = max(1, step_count - moment)
        retarded = None
        for m, piece in enumerate(later):
            term = rowwise(
                by_lag[offsets[m] : offsets[m + 1], first - 1 :],
                piece[:, moment + first - step_count : moment + lag_count + 1 - step_count],
            )
            retarded = term if retarded is None else retarded + term
        for delay in range(1, first):
            for low, high, piece in newer[moment + delay]:
                retarded = retarded + rowwise(recent[low:high, delay - 1], piece)
        current = advance(moment, retarded)
        results[moment] = current
        if moment > 0:
            pieces, new_blocks = gather_blocks(current.astype(jnp.bfloat16), wide, True)
            bounds = np.cumsum([0] + [piece.shape[0] for piece in pieces])
            newer[moment] = [
                (bounds[k], bounds[k + 1], piece) for k, piece in enumerate(pieces)
            ]
            if recent is None:
                recent = tiles_by_lag(
                    retarded_tiles,
                    tile_lags,
                    column_of_block,
                    new_blocks,
                    range(1, min(lag_count, step_count - 1) + 1),
                )
    return jnp.stack(results)


def solution(mesh):
    in_specs = (
        P(("groups", "wide"), None, None, None, None),
        P(("groups", "wide"), None, None),
        P("groups"),
        P(None, ("groups", "wide"), None),
        P(None, ("groups", "wide"), None),
        P(("groups", "wide"), None, None),
    )
    out_specs = P(None, ("groups", "wide"), None)
    return jax.shard_map(
        functools.partial(per_device, mesh.shape["wide"]),
        mesh=mesh,
        in_specs=in_specs,
        out_specs=out_specs,
        check_vma=False,
    )
```

```python
import functools

import jax
import jax.numpy as jnp
import numpy as np
from jax import lax
from jax.sharding import PartitionSpec as P


def inner_size(wide):
    for size in (4, 2):
        if wide % size == 0:
            return size
    return 1


def line_stage(x, wide, inner):
    lines = wide // inner
    if lines <= 4:
        parts = [x[None]]
        for shift in range(1, lines):
            pairs = [
                (d, ((d // inner + shift) % lines) * inner + d % inner) for d in range(wide)
            ]
            parts.append(lax.ppermute(x, "wide", pairs)[None])
        return parts, True
    groups = [[z * inner + k for z in range(lines)] for k in range(inner)]
    return [lax.all_gather(x, "wide", axis=0, tiled=False, axis_index_groups=groups)], False


def swap(x, wide, mask):
    return lax.ppermute(x, "wide", [(d, d ^ mask) for d in range(wide)])


def slab_stage(parts, wide, inner, early, split):
    stack = parts[0] if len(parts) == 1 else jnp.concatenate(parts)
    if inner != 4:
        return [stack] + [swap(stack, wide, m) for m in range(1, inner)]
    if early and len(parts) > 1:
        across = [swap(parts[0], wide, 2)]
        if split and len(parts) > 2:
            chunks = [parts[1], jnp.concatenate(parts[2:])]
        else:
            chunks = [jnp.concatenate(parts[1:])]
        across += [swap(chunk, wide, 2) for chunk in chunks]
        return [stack, swap(stack, wide, 1)] + across + [swap(piece, wide, 1) for piece in across]
    across = swap(stack, wide, 2)
    return [stack, swap(stack, wide, 1), across, swap(across, wide, 1)]


def gather_blocks(x, wide, early, split=False):
    inner = inner_size(wide)
    lines = wide // inner
    parts, shifted = line_stage(x, wide, inner)
    pieces = slab_stage(parts, wide, inner, early, split)
    me = lax.axis_index("wide")
    line = np.arange(lines, dtype=np.int32)
    source_line = (me // inner - line) % lines if shifted else jnp.asarray(line)
    masks = np.arange(inner, dtype=np.int32)
    blocks = (
        source_line[None, :] * inner
        + jnp.bitwise_xor(me % inner, jnp.asarray(masks))[:, None]
    )
    return pieces, blocks.reshape(wide)


def tiles_by_lag(retarded_tiles, tile_lags, column_of_block, block_of_slot, lags_wanted):
    columns = jnp.take(column_of_block, block_of_slot, axis=0)
    tiles = jnp.take(retarded_tiles[0], columns, axis=0)
    lags = jnp.take(tile_lags[0], columns, axis=0)
    zero = jnp.zeros_like(tiles[:, 0])
    return jnp.stack(
        [
            jnp.where(
                (lags[:, 0] == lag)[:, None, None],
                tiles[:, 0],
                jnp.where((lags[:, 1] == lag)[:, None, None], tiles[:, 1], zero),
            )
            for lag in lags_wanted
        ],
        axis=1,
    )


def rowwise(tiles, currents):
    spec = "slpq,slpr->qr" if tiles.ndim == 4 else "spq,spr->qr"
    return jnp.einsum(spec, tiles, currents, preferred_element_type=jnp.float32)


def per_device(wide, retarded_tiles, tile_lags, block_owner, later_current, excitation, inverse_blocks):
    lag_count = later_current.shape[0]
    step_count = excitation.shape[0]
    column_of_block = jnp.argsort(block_owner)

    later, later_blocks = gather_blocks(later_current, wide, True, split=True)
    offsets = np.cumsum([0] + [piece.shape[0] for piece in later])
    by_lag = tiles_by_lag(
        retarded_tiles, tile_lags, column_of_block, later_blocks, range(1, lag_count + 1)
    )
    inverse_t = inverse_blocks[0].T

    def advance(moment, retarded):
        source = excitation[moment] - retarded
        return jnp.dot(
            inverse_t, source, precision=lax.Precision.HIGHEST, preferred_element_type=jnp.float32
        )

    results = [None] * step_count
    newer = {}
    recent = None
    for moment in range(step_count - 1, -1, -1):
        first = max(1, step_count - moment)
        retarded = None
        for m, piece in enumerate(later):
            term = rowwise(
                by_lag[offsets[m] : offsets[m + 1], first - 1 :],
                piece[:, moment + first - step_count : moment + lag_count + 1 - step_count],
            )
            retarded = term if retarded is None else retarded + term
        for delay in range(1, first):
            retarded = retarded + rowwise(recent[:, delay - 1], newer[moment + delay])
        current = advance(moment, retarded)
        results[moment] = current
        if moment > 0:
            pieces, new_blocks = gather_blocks(current.astype(jnp.bfloat16), wide, True)
            newer[moment] = jnp.concatenate(pieces)
            if recent is None:
                recent = tiles_by_lag(
                    retarded_tiles,
                    tile_lags,
                    column_of_block,
                    new_blocks,
                    range(1, min(lag_count, step_count - 1) + 1),
                )
    return jnp.stack(results)


def solution(mesh):
    in_specs = (
        P(("groups", "wide"), None, None, None, None),
        P(("groups", "wide"), None, None),
        P("groups"),
        P(None, ("groups", "wide"), None),
        P(None, ("groups", "wide"), None),
        P(("groups", "wide"), None, None),
    )
    out_specs = P(None, ("groups", "wide"), None)
    return jax.shard_map(
        functools.partial(per_device, mesh.shape["wide"]),
        mesh=mesh,
        in_specs=in_specs,
        out_specs=out_specs,
        check_vma=False,
    )
```

```python
import functools

import jax
import jax.numpy as jnp
import numpy as np
from jax import lax
from jax.experimental.layout import Layout, with_layout_constraint
from jax.sharding import PartitionSpec as P


def inner_size(wide):
    for size in (4, 2):
        if wide % size == 0:
            return size
    return 1


def line_stage(x, wide, inner):
    lines = wide // inner
    if lines <= 4:
        parts = [x[None]]
        for shift in range(1, lines):
            pairs = [
                (d, ((d // inner + shift) % lines) * inner + d % inner) for d in range(wide)
            ]
            parts.append(lax.ppermute(x, "wide", pairs)[None])
        return parts, True
    groups = [[z * inner + k for z in range(lines)] for k in range(inner)]
    return [lax.all_gather(x, "wide", axis=0, tiled=False, axis_index_groups=groups)], False


def swap(x, wide, mask):
    return lax.ppermute(x, "wide", [(d, d ^ mask) for d in range(wide)])


def slab_stage(parts, wide, inner, early, split):
    stack = parts[0] if len(parts) == 1 else jnp.concatenate(parts)
    if inner != 4:
        return [stack] + [swap(stack, wide, m) for m in range(1, inner)]
    if early and len(parts) > 1:
        across = [swap(parts[0], wide, 2)]
        if split and len(parts) > 2:
            chunks = [parts[1], jnp.concatenate(parts[2:])]
        else:
            chunks = [jnp.concatenate(parts[1:])]
        across += [swap(chunk, wide, 2) for chunk in chunks]
        return [stack, swap(stack, wide, 1)] + across + [swap(piece, wide, 1) for piece in across]
    across = swap(stack, wide, 2)
    return [stack, swap(stack, wide, 1), across, swap(across, wide, 1)]


def gather_blocks(x, wide, early, split=False):
    inner = inner_size(wide)
    lines = wide // inner
    parts, shifted = line_stage(x, wide, inner)
    pieces = slab_stage(parts, wide, inner, early, split)
    me = lax.axis_index("wide")
    line = np.arange(lines, dtype=np.int32)
    source_line = (me // inner - line) % lines if shifted else jnp.asarray(line)
    masks = np.arange(inner, dtype=np.int32)
    blocks = (
        source_line[None, :] * inner
        + jnp.bitwise_xor(me % inner, jnp.asarray(masks))[:, None]
    )
    return pieces, blocks.reshape(wide)


def tiles_by_lag(retarded_tiles, tile_lags, column_of_block, block_of_slot, lags_wanted):
    columns = jnp.take(column_of_block, block_of_slot, axis=0)
    tiles = jnp.take(retarded_tiles[0], columns, axis=0)
    lags = jnp.take(tile_lags[0], columns, axis=0)
    zero = jnp.zeros_like(tiles[:, 0])
    return jnp.stack(
        [
            jnp.where(
                (lags[:, 0] == lag)[:, None, None],
                tiles[:, 0],
                jnp.where((lags[:, 1] == lag)[:, None, None], tiles[:, 1], zero),
            )
            for lag in lags_wanted
        ],
        axis=1,
    )


def rowwise(tiles, currents):
    spec = "slpq,slpr->qr" if tiles.ndim == 4 else "spq,spr->qr"
    return jnp.einsum(spec, tiles, currents, preferred_element_type=jnp.float32)


def per_device(wide, retarded_tiles, tile_lags, block_owner, later_current, excitation, inverse_blocks):
    lag_count = later_current.shape[0]
    step_count = excitation.shape[0]
    column_of_block = jnp.argsort(block_owner)

    later, later_blocks = gather_blocks(later_current, wide, True, split=True)
    offsets = np.cumsum([0] + [piece.shape[0] for piece in later])
    by_lag = tiles_by_lag(
        retarded_tiles, tile_lags, column_of_block, later_blocks, range(1, lag_count + 1)
    )
    inverse_t = inverse_blocks[0].T

    def advance(moment, retarded):
        source = excitation[moment] - retarded
        return with_layout_constraint(jnp.dot(
            inverse_t, source, precision=lax.Precision.HIGHEST, preferred_element_type=jnp.float32
        ), Layout((0, 1)))

    results = [None] * step_count
    newer = {}
    recent = None
    for moment in range(step_count - 1, -1, -1):
        first = max(1, step_count - moment)
        retarded = None
        for m, piece in enumerate(later):
            term = rowwise(
                by_lag[offsets[m] : offsets[m + 1], first - 1 :],
                piece[:, moment + first - step_count : moment + lag_count + 1 - step_count],
            )
            retarded = term if retarded is None else retarded + term
        for delay in range(1, first):
            retarded = retarded + rowwise(recent[:, delay - 1], newer[moment + delay])
        current = advance(moment, retarded)
        results[moment] = current
        if moment > 0:
            pieces, new_blocks = gather_blocks(current.astype(jnp.bfloat16), wide, True)
            newer[moment] = jnp.concatenate(pieces)
            if recent is None:
                recent = tiles_by_lag(
                    retarded_tiles,
                    tile_lags,
                    column_of_block,
                    new_blocks,
                    range(1, min(lag_count, step_count - 1) + 1),
                )
    return jnp.stack(results)


def solution(mesh):
    in_specs = (
        P(("groups", "wide"), None, None, None, None),
        P(("groups", "wide"), None, None),
        P("groups"),
        P(None, ("groups", "wide"), None),
        P(None, ("groups", "wide"), None),
        P(("groups", "wide"), None, None),
    )
    out_specs = P(None, ("groups", "wide"), None)
    return jax.shard_map(
        functools.partial(per_device, mesh.shape["wide"]),
        mesh=mesh,
        in_specs=in_specs,
        out_specs=out_specs,
        check_vma=False,
    )
```

```python
import functools

import jax
import jax.numpy as jnp
import numpy as np
from jax import lax
from jax.experimental.layout import Layout, with_layout_constraint
from jax.sharding import PartitionSpec as P


def inner_size(wide):
    for size in (4, 2):
        if wide % size == 0:
            return size
    return 1


def line_stage(x, wide, inner):
    lines = wide // inner
    if lines <= 4:
        parts = [x[None]]
        for shift in range(1, lines):
            pairs = [
                (d, ((d // inner + shift) % lines) * inner + d % inner) for d in range(wide)
            ]
            parts.append(lax.ppermute(x, "wide", pairs)[None])
        return parts, True
    groups = [[z * inner + k for z in range(lines)] for k in range(inner)]
    return [lax.all_gather(x, "wide", axis=0, tiled=False, axis_index_groups=groups)], False


def swap(x, wide, mask):
    return lax.ppermute(x, "wide", [(d, d ^ mask) for d in range(wide)])


def slab_stage(parts, wide, inner, early, split):
    stack = parts[0] if len(parts) == 1 else jnp.concatenate(parts)
    if inner != 4:
        return [stack] + [swap(stack, wide, m) for m in range(1, inner)]
    if early and len(parts) > 1:
        across = [swap(parts[0], wide, 2)]
        if split and len(parts) > 2:
            chunks = [parts[1], jnp.concatenate(parts[2:])]
        else:
            chunks = [jnp.concatenate(parts[1:])]
        across += [swap(chunk, wide, 2) for chunk in chunks]
        return [stack, swap(stack, wide, 1)] + across + [swap(piece, wide, 1) for piece in across]
    across = swap(stack, wide, 2)
    return [stack, swap(stack, wide, 1), across, swap(across, wide, 1)]


def gather_blocks(x, wide, early, split=False):
    inner = inner_size(wide)
    lines = wide // inner
    parts, shifted = line_stage(x, wide, inner)
    pieces = slab_stage(parts, wide, inner, early, split)
    me = lax.axis_index("wide")
    line = np.arange(lines, dtype=np.int32)
    source_line = (me // inner - line) % lines if shifted else jnp.asarray(line)
    masks = np.arange(inner, dtype=np.int32)
    blocks = (
        source_line[None, :] * inner
        + jnp.bitwise_xor(me % inner, jnp.asarray(masks))[:, None]
    )
    return pieces, blocks.reshape(wide)


def tiles_by_lag(retarded_tiles, tile_lags, column_of_block, block_of_slot, lags_wanted):
    columns = jnp.take(column_of_block, block_of_slot, axis=0)
    tiles = jnp.take(retarded_tiles[0], columns, axis=0)
    lags = jnp.take(tile_lags[0], columns, axis=0)
    zero = jnp.zeros_like(tiles[:, 0])
    return jnp.stack(
        [
            jnp.where(
                (lags[:, 0] == lag)[:, None, None],
                tiles[:, 0],
                jnp.where((lags[:, 1] == lag)[:, None, None], tiles[:, 1], zero),
            )
            for lag in lags_wanted
        ],
        axis=1,
    )


def rowwise(tiles, currents):
    spec = "slpq,slpr->qr" if tiles.ndim == 4 else "spq,spr->qr"
    return jnp.einsum(spec, tiles, currents, preferred_element_type=jnp.float32)


def per_device(wide, retarded_tiles, tile_lags, block_owner, later_current, excitation, inverse_blocks):
    lag_count = later_current.shape[0]
    step_count = excitation.shape[0]
    column_of_block = jnp.argsort(block_owner)

    later, later_blocks = gather_blocks(later_current, wide, True, split=True)
    offsets = np.cumsum([0] + [piece.shape[0] for piece in later])
    by_lag = tiles_by_lag(
        retarded_tiles, tile_lags, column_of_block, later_blocks, range(1, lag_count + 1)
    )
    inverse_t = inverse_blocks[0].T

    def advance(moment, retarded):
        source = excitation[moment] - retarded
        return with_layout_constraint(jnp.dot(
            inverse_t, source, precision=lax.Precision.HIGHEST, preferred_element_type=jnp.float32
        ), Layout((0, 1)))

    output = jnp.zeros((step_count,) + excitation.shape[1:], jnp.float32)
    newer = {}
    recent = None
    for moment in range(step_count - 1, -1, -1):
        first = max(1, step_count - moment)
        retarded = None
        for m, piece in enumerate(later):
            term = rowwise(
                by_lag[offsets[m] : offsets[m + 1], first - 1 :],
                piece[:, moment + first - step_count : moment + lag_count + 1 - step_count],
            )
            retarded = term if retarded is None else retarded + term
        for delay in range(1, first):
            retarded = retarded + rowwise(recent[:, delay - 1], newer[moment + delay])
        current = advance(moment, retarded)
        output = lax.dynamic_update_slice(output, current[None], (moment, 0, 0))
        if moment > 0:
            pieces, new_blocks = gather_blocks(current.astype(jnp.bfloat16), wide, True)
            newer[moment] = jnp.concatenate(pieces)
            if recent is None:
                recent = tiles_by_lag(
                    retarded_tiles,
                    tile_lags,
                    column_of_block,
                    new_blocks,
                    range(1, min(lag_count, step_count - 1) + 1),
                )
    return output


def solution(mesh):
    in_specs = (
        P(("groups", "wide"), None, None, None, None),
        P(("groups", "wide"), None, None),
        P("groups"),
        P(None, ("groups", "wide"), None),
        P(None, ("groups", "wide"), None),
        P(("groups", "wide"), None, None),
    )
    out_specs = P(None, ("groups", "wide"), None)
    return jax.shard_map(
        functools.partial(per_device, mesh.shape["wide"]),
        mesh=mesh,
        in_specs=in_specs,
        out_specs=out_specs,
        check_vma=False,
    )
```

```python
import functools

import jax
import jax.numpy as jnp
import numpy as np
from jax import lax
from jax.experimental.layout import Layout, with_layout_constraint
from jax.sharding import PartitionSpec as P


def inner_size(wide):
    for size in (4, 2):
        if wide % size == 0:
            return size
    return 1


def line_stage(x, wide, inner):
    lines = wide // inner
    if lines <= 4:
        parts = [x[None]]
        for shift in range(1, lines):
            pairs = [
                (d, ((d // inner + shift) % lines) * inner + d % inner) for d in range(wide)
            ]
            parts.append(lax.ppermute(x, "wide", pairs)[None])
        return parts, True
    groups = [[z * inner + k for z in range(lines)] for k in range(inner)]
    return [lax.all_gather(x, "wide", axis=0, tiled=False, axis_index_groups=groups)], False


def swap(x, wide, mask):
    return lax.ppermute(x, "wide", [(d, d ^ mask) for d in range(wide)])


def slab_stage(parts, wide, inner, early, split):
    stack = parts[0] if len(parts) == 1 else jnp.concatenate(parts)
    if inner != 4:
        return [stack] + [swap(stack, wide, m) for m in range(1, inner)]
    if early and len(parts) > 1:
        across = [swap(parts[0], wide, 2)]
        if split and len(parts) > 2:
            chunks = parts[1:]
        else:
            chunks = [jnp.concatenate(parts[1:])]
        across += [swap(chunk, wide, 2) for chunk in chunks]
        return [stack, swap(stack, wide, 1)] + across + [swap(piece, wide, 1) for piece in across]
    across = swap(stack, wide, 2)
    return [stack, swap(stack, wide, 1), across, swap(across, wide, 1)]


def gather_blocks(x, wide, early, split=False):
    inner = inner_size(wide)
    lines = wide // inner
    parts, shifted = line_stage(x, wide, inner)
    pieces = slab_stage(parts, wide, inner, early, split)
    me = lax.axis_index("wide")
    line = np.arange(lines, dtype=np.int32)
    source_line = (me // inner - line) % lines if shifted else jnp.asarray(line)
    masks = np.arange(inner, dtype=np.int32)
    blocks = (
        source_line[None, :] * inner
        + jnp.bitwise_xor(me % inner, jnp.asarray(masks))[:, None]
    )
    return pieces, blocks.reshape(wide)


def tiles_by_lag(retarded_tiles, tile_lags, column_of_block, block_of_slot, lags_wanted):
    columns = jnp.take(column_of_block, block_of_slot, axis=0)
    tiles = jnp.take(retarded_tiles[0], columns, axis=0)
    lags = jnp.take(tile_lags[0], columns, axis=0)
    zero = jnp.zeros_like(tiles[:, 0])
    return jnp.stack(
        [
            jnp.where(
                (lags[:, 0] == lag)[:, None, None],
                tiles[:, 0],
                jnp.where((lags[:, 1] == lag)[:, None, None], tiles[:, 1], zero),
            )
            for lag in lags_wanted
        ],
        axis=1,
    )


def rowwise(tiles, currents):
    spec = "slpq,slpr->qr" if tiles.ndim == 4 else "spq,spr->qr"
    return jnp.einsum(spec, tiles, currents, preferred_element_type=jnp.float32)


def per_device(wide, retarded_tiles, tile_lags, block_owner, later_current, excitation, inverse_blocks):
    lag_count = later_current.shape[0]
    step_count = excitation.shape[0]
    column_of_block = jnp.argsort(block_owner)

    later, later_blocks = gather_blocks(later_current, wide, True, split=True)
    offsets = np.cumsum([0] + [piece.shape[0] for piece in later])
    by_lag = tiles_by_lag(
        retarded_tiles, tile_lags, column_of_block, later_blocks, range(1, lag_count + 1)
    )
    inverse_t = inverse_blocks[0].T

    def advance(moment, retarded):
        source = excitation[moment] - retarded
        return with_layout_constraint(jnp.dot(
            inverse_t, source, precision=lax.Precision.HIGHEST, preferred_element_type=jnp.float32
        ), Layout((0, 1)))

    results = [None] * step_count
    newer = {}
    recent = None
    for moment in range(step_count - 1, -1, -1):
        first = max(1, step_count - moment)
        retarded = None
        for m, piece in enumerate(later):
            term = rowwise(
                by_lag[offsets[m] : offsets[m + 1], first - 1 :],
                piece[:, moment + first - step_count : moment + lag_count + 1 - step_count],
            )
            retarded = term if retarded is None else retarded + term
        for delay in range(1, first):
            retarded = retarded + rowwise(recent[:, delay - 1], newer[moment + delay])
        current = advance(moment, retarded)
        results[moment] = current
        if moment > 0:
            pieces, new_blocks = gather_blocks(current.astype(jnp.bfloat16), wide, True)
            newer[moment] = jnp.concatenate(pieces)
            if recent is None:
                recent = tiles_by_lag(
                    retarded_tiles,
                    tile_lags,
                    column_of_block,
                    new_blocks,
                    range(1, min(lag_count, step_count - 1) + 1),
                )
    return jnp.stack(results)


def solution(mesh):
    in_specs = (
        P(("groups", "wide"), None, None, None, None),
        P(("groups", "wide"), None, None),
        P("groups"),
        P(None, ("groups", "wide"), None),
        P(None, ("groups", "wide"), None),
        P(("groups", "wide"), None, None),
    )
    out_specs = P(None, ("groups", "wide"), None)
    return jax.shard_map(
        functools.partial(per_device, mesh.shape["wide"]),
        mesh=mesh,
        in_specs=in_specs,
        out_specs=out_specs,
        check_vma=False,
    )
```

```python
import functools

import jax
import jax.numpy as jnp
import numpy as np
from jax import lax
from jax.experimental.layout import Layout, with_layout_constraint
from jax.sharding import PartitionSpec as P


def inner_size(wide):
    for size in (4, 2):
        if wide % size == 0:
            return size
    return 1


def line_stage(x, wide, inner):
    lines = wide // inner
    if lines <= 4:
        parts = [x[None]]
        for shift in range(1, lines):
            pairs = [
                (d, ((d // inner + shift) % lines) * inner + d % inner) for d in range(wide)
            ]
            parts.append(lax.ppermute(x, "wide", pairs)[None])
        return parts, True
    groups = [[z * inner + k for z in range(lines)] for k in range(inner)]
    return [lax.all_gather(x, "wide", axis=0, tiled=False, axis_index_groups=groups)], False


def swap(x, wide, mask):
    return lax.ppermute(x, "wide", [(d, d ^ mask) for d in range(wide)])


def slab_stage(parts, wide, inner, early, split):
    stack = parts[0] if len(parts) == 1 else jnp.concatenate(parts)
    if inner != 4:
        return [stack] + [swap(stack, wide, m) for m in range(1, inner)]
    if early and len(parts) > 1:
        across = [swap(parts[0], wide, 2)]
        if split and len(parts) > 2:
            chunks = [parts[1], jnp.concatenate(parts[2:])]
        else:
            chunks = [jnp.concatenate(parts[1:])]
        across += [swap(chunk, wide, 2) for chunk in chunks]
        beside = [swap(parts[0], wide, 1)]
        if split:
            beside.append(swap(jnp.concatenate(parts[1:]), wide, 1))
        else:
            beside = [swap(stack, wide, 1)]
        return [stack] + beside + across + [swap(piece, wide, 1) for piece in across]
    across = swap(stack, wide, 2)
    return [stack, swap(stack, wide, 1), across, swap(across, wide, 1)]


def gather_blocks(x, wide, early, split=False):
    inner = inner_size(wide)
    lines = wide // inner
    parts, shifted = line_stage(x, wide, inner)
    pieces = slab_stage(parts, wide, inner, early, split)
    me = lax.axis_index("wide")
    line = np.arange(lines, dtype=np.int32)
    source_line = (me // inner - line) % lines if shifted else jnp.asarray(line)
    masks = np.arange(inner, dtype=np.int32)
    blocks = (
        source_line[None, :] * inner
        + jnp.bitwise_xor(me % inner, jnp.asarray(masks))[:, None]
    )
    return pieces, blocks.reshape(wide)


def tiles_by_lag(retarded_tiles, tile_lags, column_of_block, block_of_slot, lags_wanted):
    columns = jnp.take(column_of_block, block_of_slot, axis=0)
    tiles = jnp.take(retarded_tiles[0], columns, axis=0)
    lags = jnp.take(tile_lags[0], columns, axis=0)
    zero = jnp.zeros_like(tiles[:, 0])
    return jnp.stack(
        [
            jnp.where(
                (lags[:, 0] == lag)[:, None, None],
                tiles[:, 0],
                jnp.where((lags[:, 1] == lag)[:, None, None], tiles[:, 1], zero),
            )
            for lag in lags_wanted
        ],
        axis=1,
    )


def rowwise(tiles, currents):
    spec = "slpq,slpr->qr" if tiles.ndim == 4 else "spq,spr->qr"
    return jnp.einsum(spec, tiles, currents, preferred_element_type=jnp.float32)


def per_device(wide, retarded_tiles, tile_lags, block_owner, later_current, excitation, inverse_blocks):
    lag_count = later_current.shape[0]
    step_count = excitation.shape[0]
    column_of_block = jnp.argsort(block_owner)

    later, later_blocks = gather_blocks(later_current, wide, True, split=True)
    offsets = np.cumsum([0] + [piece.shape[0] for piece in later])
    by_lag = tiles_by_lag(
        retarded_tiles, tile_lags, column_of_block, later_blocks, range(1, lag_count + 1)
    )
    inverse_t = inverse_blocks[0].T

    def advance(moment, retarded):
        source = excitation[moment] - retarded
        return with_layout_constraint(jnp.dot(
            inverse_t, source, precision=lax.Precision.HIGHEST, preferred_element_type=jnp.float32
        ), Layout((0, 1)))

    results = [None] * step_count
    newer = {}
    recent = None
    for moment in range(step_count - 1, -1, -1):
        first = max(1, step_count - moment)
        retarded = None
        for m, piece in enumerate(later):
            term = rowwise(
                by_lag[offsets[m] : offsets[m + 1], first - 1 :],
                piece[:, moment + first - step_count : moment + lag_count + 1 - step_count],
            )
            retarded = term if retarded is None else retarded + term
        for delay in range(1, first):
            retarded = retarded + rowwise(recent[:, delay - 1], newer[moment + delay])
        current = advance(moment, retarded)
        results[moment] = current
        if moment > 0:
            pieces, new_blocks = gather_blocks(current.astype(jnp.bfloat16), wide, True)
            newer[moment] = jnp.concatenate(pieces)
            if recent is None:
                recent = tiles_by_lag(
                    retarded_tiles,
                    tile_lags,
                    column_of_block,
                    new_blocks,
                    range(1, min(lag_count, step_count - 1) + 1),
                )
    return jnp.stack(results)


def solution(mesh):
    in_specs = (
        P(("groups", "wide"), None, None, None, None),
        P(("groups", "wide"), None, None),
        P("groups"),
        P(None, ("groups", "wide"), None),
        P(None, ("groups", "wide"), None),
        P(("groups", "wide"), None, None),
    )
    out_specs = P(None, ("groups", "wide"), None)
    return jax.shard_map(
        functools.partial(per_device, mesh.shape["wide"]),
        mesh=mesh,
        in_specs=in_specs,
        out_specs=out_specs,
        check_vma=False,
    )
```

```python
import functools

import jax
import jax.numpy as jnp
import numpy as np
from jax import lax
from jax.experimental.layout import Layout, with_layout_constraint
from jax.sharding import PartitionSpec as P


def inner_size(wide):
    for size in (4, 2):
        if wide % size == 0:
            return size
    return 1


def line_stage(x, wide, inner):
    lines = wide // inner
    if lines <= 4:
        paired = (lines & (lines - 1)) == 0
        parts = [x[None]]
        for shift in range(1, lines):
            pairs = [
                (d, ((d // inner ^ shift) if paired else (d // inner + shift) % lines) * inner + d % inner)
                for d in range(wide)
            ]
            parts.append(lax.ppermute(x, "wide", pairs)[None])
        return parts, "paired" if paired else "shifted"
    groups = [[z * inner + k for z in range(lines)] for k in range(inner)]
    return [lax.all_gather(x, "wide", axis=0, tiled=False, axis_index_groups=groups)], "ordered"


def swap(x, wide, mask):
    return lax.ppermute(x, "wide", [(d, d ^ mask) for d in range(wide)])


def slab_stage(parts, wide, inner, early, split):
    stack = parts[0] if len(parts) == 1 else jnp.concatenate(parts)
    if inner != 4:
        return [stack] + [swap(stack, wide, m) for m in range(1, inner)]
    if early and len(parts) > 1:
        across = [swap(parts[0], wide, 2)]
        if split and len(parts) > 2:
            chunks = [parts[1], jnp.concatenate(parts[2:])]
        else:
            chunks = [jnp.concatenate(parts[1:])]
        across += [swap(chunk, wide, 2) for chunk in chunks]
        return [stack, swap(stack, wide, 1)] + across + [swap(piece, wide, 1) for piece in across]
    across = swap(stack, wide, 2)
    return [stack, swap(stack, wide, 1), across, swap(across, wide, 1)]


def gather_blocks(x, wide, early, split=False):
    inner = inner_size(wide)
    lines = wide // inner
    parts, shifted = line_stage(x, wide, inner)
    pieces = slab_stage(parts, wide, inner, early, split)
    me = lax.axis_index("wide")
    line = np.arange(lines, dtype=np.int32)
    if shifted == "paired":
        source_line = jnp.bitwise_xor(me // inner, jnp.asarray(line))
    elif shifted == "shifted":
        source_line = (me // inner - line) % lines
    else:
        source_line = jnp.asarray(line)
    masks = np.arange(inner, dtype=np.int32)
    blocks = (
        source_line[None, :] * inner
        + jnp.bitwise_xor(me % inner, jnp.asarray(masks))[:, None]
    )
    return pieces, blocks.reshape(wide)


def tiles_by_lag(retarded_tiles, tile_lags, column_of_block, block_of_slot, lags_wanted):
    columns = jnp.take(column_of_block, block_of_slot, axis=0)
    tiles = jnp.take(retarded_tiles[0], columns, axis=0)
    lags = jnp.take(tile_lags[0], columns, axis=0)
    zero = jnp.zeros_like(tiles[:, 0])
    return jnp.stack(
        [
            jnp.where(
                (lags[:, 0] == lag)[:, None, None],
                tiles[:, 0],
                jnp.where((lags[:, 1] == lag)[:, None, None], tiles[:, 1], zero),
            )
            for lag in lags_wanted
        ],
        axis=1,
    )


def rowwise(tiles, currents):
    spec = "slpq,slpr->qr" if tiles.ndim == 4 else "spq,spr->qr"
    return jnp.einsum(spec, tiles, currents, preferred_element_type=jnp.float32)


def per_device(wide, retarded_tiles, tile_lags, block_owner, later_current, excitation, inverse_blocks):
    lag_count = later_current.shape[0]
    step_count = excitation.shape[0]
    column_of_block = jnp.argsort(block_owner)

    later, later_blocks = gather_blocks(later_current, wide, True, split=True)
    offsets = np.cumsum([0] + [piece.shape[0] for piece in later])
    by_lag = tiles_by_lag(
        retarded_tiles, tile_lags, column_of_block, later_blocks, range(1, lag_count + 1)
    )
    inverse_t = inverse_blocks[0].T

    def advance(moment, retarded):
        source = excitation[moment] - retarded
        return with_layout_constraint(jnp.dot(
            inverse_t, source, precision=lax.Precision.HIGHEST, preferred_element_type=jnp.float32
        ), Layout((0, 1)))

    results = [None] * step_count
    newer = {}
    recent = None
    for moment in range(step_count - 1, -1, -1):
        first = max(1, step_count - moment)
        retarded = None
        for m, piece in enumerate(later):
            term = rowwise(
                by_lag[offsets[m] : offsets[m + 1], first - 1 :],
                piece[:, moment + first - step_count : moment + lag_count + 1 - step_count],
            )
            retarded = term if retarded is None else retarded + term
        for delay in range(1, first):
            retarded = retarded + rowwise(recent[:, delay - 1], newer[moment + delay])
        current = advance(moment, retarded)
        results[moment] = current
        if moment > 0:
            pieces, new_blocks = gather_blocks(current.astype(jnp.bfloat16), wide, True)
            newer[moment] = jnp.concatenate(pieces)
            if recent is None:
                recent = tiles_by_lag(
                    retarded_tiles,
                    tile_lags,
                    column_of_block,
                    new_blocks,
                    range(1, min(lag_count, step_count - 1) + 1),
                )
    return jnp.stack(results)


def solution(mesh):
    in_specs = (
        P(("groups", "wide"), None, None, None, None),
        P(("groups", "wide"), None, None),
        P("groups"),
        P(None, ("groups", "wide"), None),
        P(None, ("groups", "wide"), None),
        P(("groups", "wide"), None, None),
    )
    out_specs = P(None, ("groups", "wide"), None)
    return jax.shard_map(
        functools.partial(per_device, mesh.shape["wide"]),
        mesh=mesh,
        in_specs=in_specs,
        out_specs=out_specs,
        check_vma=False,
    )
```

```python
import functools

import jax
import jax.numpy as jnp
import numpy as np
from jax import lax
from jax.experimental.layout import Layout, with_layout_constraint
from jax.sharding import PartitionSpec as P


def inner_size(wide):
    for size in (4, 2):
        if wide % size == 0:
            return size
    return 1


def line_stage(x, wide, inner):
    lines = wide // inner
    if lines <= 4:
        parts = [x[None]]
        for shift in range(1, lines):
            pairs = [
                (d, ((d // inner + shift) % lines) * inner + d % inner) for d in range(wide)
            ]
            parts.append(lax.ppermute(x, "wide", pairs)[None])
        return parts, True
    groups = [[z * inner + k for z in range(lines)] for k in range(inner)]
    return [lax.all_gather(x, "wide", axis=0, tiled=False, axis_index_groups=groups)], False


def swap(x, wide, mask):
    return lax.ppermute(x, "wide", [(d, d ^ mask) for d in range(wide)])


def slab_stage(parts, wide, inner, early, split):
    stack = parts[0] if len(parts) == 1 else jnp.concatenate(parts)
    if inner != 4:
        return [stack] + [swap(stack, wide, m) for m in range(1, inner)]
    if early and len(parts) > 1:
        across = [swap(parts[0], wide, 2)]
        if split and len(parts) > 2:
            across.append(swap(jnp.concatenate(parts[1:-1]), wide, 2))
            last, _ = lax.optimization_barrier((parts[-1], across[-1]))
            across.append(swap(last, wide, 2))
        else:
            across.append(swap(jnp.concatenate(parts[1:]), wide, 2))
        return [stack, swap(stack, wide, 1)] + across + [swap(piece, wide, 1) for piece in across]
    across = swap(stack, wide, 2)
    return [stack, swap(stack, wide, 1), across, swap(across, wide, 1)]


def gather_blocks(x, wide, early, split=False):
    inner = inner_size(wide)
    lines = wide // inner
    parts, shifted = line_stage(x, wide, inner)
    pieces = slab_stage(parts, wide, inner, early, split)
    me = lax.axis_index("wide")
    line = np.arange(lines, dtype=np.int32)
    source_line = (me // inner - line) % lines if shifted else jnp.asarray(line)
    masks = np.arange(inner, dtype=np.int32)
    blocks = (
        source_line[None, :] * inner
        + jnp.bitwise_xor(me % inner, jnp.asarray(masks))[:, None]
    )
    return pieces, blocks.reshape(wide)


def tiles_by_lag(retarded_tiles, tile_lags, column_of_block, block_of_slot, lags_wanted):
    columns = jnp.take(column_of_block, block_of_slot, axis=0)
    tiles = jnp.take(retarded_tiles[0], columns, axis=0)
    lags = jnp.take(tile_lags[0], columns, axis=0)
    zero = jnp.zeros_like(tiles[:, 0])
    return jnp.stack(
        [
            jnp.where(
                (lags[:, 0] == lag)[:, None, None],
                tiles[:, 0],
                jnp.where((lags[:, 1] == lag)[:, None, None], tiles[:, 1], zero),
            )
            for lag in lags_wanted
        ],
        axis=1,
    )


def rowwise(tiles, currents):
    spec = "slpq,slpr->qr" if tiles.ndim == 4 else "spq,spr->qr"
    return jnp.einsum(spec, tiles, currents, preferred_element_type=jnp.float32)


def per_device(wide, retarded_tiles, tile_lags, block_owner, later_current, excitation, inverse_blocks):
    lag_count = later_current.shape[0]
    step_count = excitation.shape[0]
    column_of_block = jnp.argsort(block_owner)

    later, later_blocks = gather_blocks(later_current, wide, True, split=True)
    offsets = np.cumsum([0] + [piece.shape[0] for piece in later])
    by_lag = tiles_by_lag(
        retarded_tiles, tile_lags, column_of_block, later_blocks, range(1, lag_count + 1)
    )
    inverse_t = inverse_blocks[0].T

    def advance(moment, retarded):
        source = excitation[moment] - retarded
        return with_layout_constraint(jnp.dot(
            inverse_t, source, precision=lax.Precision.HIGHEST, preferred_element_type=jnp.float32
        ), Layout((0, 1)))

    results = [None] * step_count
    newer = {}
    recent = None
    for moment in range(step_count - 1, -1, -1):
        first = max(1, step_count - moment)
        retarded = None
        for m, piece in enumerate(later):
            term = rowwise(
                by_lag[offsets[m] : offsets[m + 1], first - 1 :],
                piece[:, moment + first - step_count : moment + lag_count + 1 - step_count],
            )
            retarded = term if retarded is None else retarded + term
        for delay in range(1, first):
            retarded = retarded + rowwise(recent[:, delay - 1], newer[moment + delay])
        current = advance(moment, retarded)
        results[moment] = current
        if moment > 0:
            pieces, new_blocks = gather_blocks(current.astype(jnp.bfloat16), wide, True)
            newer[moment] = jnp.concatenate(pieces)
            if recent is None:
                recent = tiles_by_lag(
                    retarded_tiles,
                    tile_lags,
                    column_of_block,
                    new_blocks,
                    range(1, min(lag_count, step_count - 1) + 1),
                )
    return jnp.stack(results)


def solution(mesh):
    in_specs = (
        P(("groups", "wide"), None, None, None, None),
        P(("groups", "wide"), None, None),
        P("groups"),
        P(None, ("groups", "wide"), None),
        P(None, ("groups", "wide"), None),
        P(("groups", "wide"), None, None),
    )
    out_specs = P(None, ("groups", "wide"), None)
    return jax.shard_map(
        functools.partial(per_device, mesh.shape["wide"]),
        mesh=mesh,
        in_specs=in_specs,
        out_specs=out_specs,
        check_vma=False,
    )
```

```python
import functools

import jax
import jax.numpy as jnp
import numpy as np
from jax import lax
from jax.experimental.layout import Layout, with_layout_constraint
from jax.sharding import PartitionSpec as P


def inner_size(wide):
    for size in (4, 2):
        if wide % size == 0:
            return size
    return 1


def line_stage(x, wide, inner):
    lines = wide // inner
    if lines <= 4:
        parts = [x[None]]
        for shift in range(1, lines):
            pairs = [
                (d, ((d // inner + shift) % lines) * inner + d % inner) for d in range(wide)
            ]
            parts.append(lax.ppermute(x, "wide", pairs)[None])
        return parts, True
    groups = [[z * inner + k for z in range(lines)] for k in range(inner)]
    return [lax.all_gather(x, "wide", axis=0, tiled=False, axis_index_groups=groups)], False


def swap(x, wide, mask):
    return lax.ppermute(x, "wide", [(d, d ^ mask) for d in range(wide)])


def slab_stage(parts, wide, inner, early, split):
    stack = parts[0] if len(parts) == 1 else jnp.concatenate(parts)
    if inner != 4:
        return [stack] + [swap(stack, wide, m) for m in range(1, inner)]
    if early and len(parts) > 1:
        across = [swap(parts[0], wide, 2)]
        if split and len(parts) > 2:
            chunks = [parts[1], jnp.concatenate(parts[2:])]
        else:
            chunks = [jnp.concatenate(parts[1:])]
        across += [swap(chunk, wide, 2) for chunk in chunks]
        return [stack, swap(stack, wide, 1)] + across + [swap(piece, wide, 1) for piece in across]
    across = swap(stack, wide, 2)
    return [stack, swap(stack, wide, 1), across, swap(across, wide, 1)]


def gather_blocks(x, wide, early, split=False):
    inner = inner_size(wide)
    lines = wide // inner
    parts, shifted = line_stage(x, wide, inner)
    pieces = slab_stage(parts, wide, inner, early, split)
    me = lax.axis_index("wide")
    line = np.arange(lines, dtype=np.int32)
    source_line = (me // inner - line) % lines if shifted else jnp.asarray(line)
    masks = np.arange(inner, dtype=np.int32)
    blocks = (
        source_line[None, :] * inner
        + jnp.bitwise_xor(me % inner, jnp.asarray(masks))[:, None]
    )
    return pieces, blocks.reshape(wide)


def tiles_by_lag(retarded_tiles, tile_lags, column_of_block, block_of_slot, lags_wanted):
    columns = jnp.take(column_of_block, block_of_slot, axis=0)
    tiles = jnp.take(retarded_tiles[0], columns, axis=0)
    lags = jnp.take(tile_lags[0], columns, axis=0)
    zero = jnp.zeros_like(tiles[:, 0])
    return jnp.stack(
        [
            jnp.where(
                (lags[:, 0] == lag)[:, None, None],
                tiles[:, 0],
                jnp.where((lags[:, 1] == lag)[:, None, None], tiles[:, 1], zero),
            )
            for lag in lags_wanted
        ],
        axis=1,
    )


def rowwise(tiles, currents):
    spec = "slpq,slpr->qr" if tiles.ndim == 4 else "spq,spr->qr"
    return jnp.einsum(spec, tiles, currents, preferred_element_type=jnp.float32)


def per_device(wide, retarded_tiles, tile_lags, block_owner, later_current, excitation, inverse_blocks):
    lag_count = later_current.shape[0]
    step_count = excitation.shape[0]
    column_of_block = jnp.argsort(block_owner)

    later, later_blocks = gather_blocks(later_current, wide, True, split=True)
    offsets = np.cumsum([0] + [piece.shape[0] for piece in later])
    by_lag = tiles_by_lag(
        retarded_tiles, tile_lags, column_of_block, later_blocks, range(1, lag_count + 1)
    )
    inverse_t = inverse_blocks[0].T

    def advance(moment, retarded):
        source = excitation[moment] - retarded
        return with_layout_constraint(jnp.dot(
            inverse_t, source, precision=lax.Precision.HIGH, preferred_element_type=jnp.float32
        ), Layout((0, 1)))

    results = [None] * step_count
    newer = {}
    recent = None
    for moment in range(step_count - 1, -1, -1):
        first = max(1, step_count - moment)
        retarded = None
        for m, piece in enumerate(later):
            term = rowwise(
                by_lag[offsets[m] : offsets[m + 1], first - 1 :],
                piece[:, moment + first - step_count : moment + lag_count + 1 - step_count],
            )
            retarded = term if retarded is None else retarded + term
        for delay in range(1, first):
            retarded = retarded + rowwise(recent[:, delay - 1], newer[moment + delay])
        current = advance(moment, retarded)
        results[moment] = current
        if moment > 0:
            pieces, new_blocks = gather_blocks(current.astype(jnp.bfloat16), wide, True)
            newer[moment] = jnp.concatenate(pieces)
            if recent is None:
                recent = tiles_by_lag(
                    retarded_tiles,
                    tile_lags,
                    column_of_block,
                    new_blocks,
                    range(1, min(lag_count, step_count - 1) + 1),
                )
    return jnp.stack(results)


def solution(mesh):
    in_specs = (
        P(("groups", "wide"), None, None, None, None),
        P(("groups", "wide"), None, None),
        P("groups"),
        P(None, ("groups", "wide"), None),
        P(None, ("groups", "wide"), None),
        P(("groups", "wide"), None, None),
    )
    out_specs = P(None, ("groups", "wide"), None)
    return jax.shard_map(
        functools.partial(per_device, mesh.shape["wide"]),
        mesh=mesh,
        in_specs=in_specs,
        out_specs=out_specs,
        check_vma=False,
    )
```

```python
import functools

import jax
import jax.numpy as jnp
import numpy as np
from jax import lax
from jax.experimental.layout import Layout, with_layout_constraint
from jax.sharding import PartitionSpec as P


def inner_size(wide):
    for size in (4, 2):
        if wide % size == 0:
            return size
    return 1


def line_stage(x, wide, inner):
    lines = wide // inner
    if lines <= 4:
        parts = [x[None]]
        for shift in range(1, lines):
            pairs = [
                (d, ((d // inner + shift) % lines) * inner + d % inner) for d in range(wide)
            ]
            parts.append(lax.ppermute(x, "wide", pairs)[None])
        return parts, True
    groups = [[z * inner + k for z in range(lines)] for k in range(inner)]
    return [lax.all_gather(x, "wide", axis=0, tiled=False, axis_index_groups=groups)], False


def swap(x, wide, mask):
    return lax.ppermute(x, "wide", [(d, d ^ mask) for d in range(wide)])


def slab_stage(parts, wide, inner, early, split):
    stack = parts[0] if len(parts) == 1 else jnp.concatenate(parts)
    if inner != 4:
        return [stack] + [swap(stack, wide, m) for m in range(1, inner)]
    if early and len(parts) > 1:
        across = [swap(parts[0], wide, 2)]
        if split and len(parts) > 2:
            chunks = [parts[1], jnp.concatenate(parts[2:])]
        else:
            chunks = [jnp.concatenate(parts[1:])]
        across += [swap(chunk, wide, 2) for chunk in chunks]
        return [stack, swap(stack, wide, 1)] + across + [swap(piece, wide, 1) for piece in across]
    across = swap(stack, wide, 2)
    return [stack, swap(stack, wide, 1), across, swap(across, wide, 1)]


def gather_blocks(x, wide, early, split=False):
    inner = inner_size(wide)
    lines = wide // inner
    parts, shifted = line_stage(x, wide, inner)
    pieces = slab_stage(parts, wide, inner, early, split)
    me = lax.axis_index("wide")
    line = np.arange(lines, dtype=np.int32)
    source_line = (me // inner - line) % lines if shifted else jnp.asarray(line)
    masks = np.arange(inner, dtype=np.int32)
    blocks = (
        source_line[None, :] * inner
        + jnp.bitwise_xor(me % inner, jnp.asarray(masks))[:, None]
    )
    return pieces, blocks.reshape(wide)


def tiles_by_lag(retarded_tiles, tile_lags, column_of_block, block_of_slot, lags_wanted):
    columns = jnp.take(column_of_block, block_of_slot, axis=0)
    tiles = jnp.take(retarded_tiles[0], columns, axis=0)
    lags = jnp.take(tile_lags[0], columns, axis=0)
    zero = jnp.zeros_like(tiles[:, 0])
    return jnp.stack(
        [
            jnp.where(
                (lags[:, 0] == lag)[:, None, None],
                tiles[:, 0],
                jnp.where((lags[:, 1] == lag)[:, None, None], tiles[:, 1], zero),
            )
            for lag in lags_wanted
        ],
        axis=1,
    )


def rowwise(tiles, currents):
    spec = "slpq,slpr->qr" if tiles.ndim == 4 else "spq,spr->qr"
    return jnp.einsum(spec, tiles, currents, preferred_element_type=jnp.float32)


def per_device(wide, retarded_tiles, tile_lags, block_owner, later_current, excitation, inverse_blocks):
    lag_count = later_current.shape[0]
    step_count = excitation.shape[0]
    column_of_block = jnp.argsort(block_owner)

    later, later_blocks = gather_blocks(later_current, wide, True, split=True)
    offsets = np.cumsum([0] + [piece.shape[0] for piece in later])
    by_lag = tiles_by_lag(
        retarded_tiles, tile_lags, column_of_block, later_blocks, range(1, lag_count + 1)
    )
    inverse_t = inverse_blocks[0].T

    def advance(moment, retarded):
        source = excitation[moment] - retarded
        return with_layout_constraint(jnp.dot(
            inverse_t, source, precision=lax.Precision.HIGHEST, preferred_element_type=jnp.float32
        ), Layout((0, 1)))

    results = [None] * step_count
    newer = {}
    recent = None
    for moment in range(step_count - 1, -1, -1):
        first = max(1, step_count - moment)
        retarded = None
        for m, piece in enumerate(later):
            term = rowwise(
                by_lag[offsets[m] : offsets[m + 1], first - 1 :],
                piece[:, moment + first - step_count : moment + lag_count + 1 - step_count],
            )
            retarded = term if retarded is None else retarded + term
        for delay in range(1, first):
            retarded = retarded + rowwise(recent[:, delay - 1], newer[moment + delay])
        current = advance(moment, retarded)
        results[moment] = current
        if moment > 0:
            pieces, new_blocks = gather_blocks(current.astype(jnp.bfloat16), wide, True, split=True)
            newer[moment] = jnp.concatenate(pieces)
            if recent is None:
                recent = tiles_by_lag(
                    retarded_tiles,
                    tile_lags,
                    column_of_block,
                    new_blocks,
                    range(1, min(lag_count, step_count - 1) + 1),
                )
    return jnp.stack(results)


def solution(mesh):
    in_specs = (
        P(("groups", "wide"), None, None, None, None),
        P(("groups", "wide"), None, None),
        P("groups"),
        P(None, ("groups", "wide"), None),
        P(None, ("groups", "wide"), None),
        P(("groups", "wide"), None, None),
    )
    out_specs = P(None, ("groups", "wide"), None)
    return jax.shard_map(
        functools.partial(per_device, mesh.shape["wide"]),
        mesh=mesh,
        in_specs=in_specs,
        out_specs=out_specs,
        check_vma=False,
    )
```

```python
import functools

import jax
import jax.numpy as jnp
import numpy as np
from jax import lax
from jax.experimental.layout import Layout, with_layout_constraint
from jax.sharding import PartitionSpec as P


def inner_size(wide):
    for size in (4, 2):
        if wide % size == 0:
            return size
    return 1


def line_stage(x, wide, inner):
    lines = wide // inner
    if lines <= 4:
        parts = [x[None]]
        for shift in range(1, lines):
            pairs = [
                (d, ((d // inner + shift) % lines) * inner + d % inner) for d in range(wide)
            ]
            parts.append(lax.ppermute(x, "wide", pairs)[None])
        return parts, True
    groups = [[z * inner + k for z in range(lines)] for k in range(inner)]
    return [lax.all_gather(x, "wide", axis=0, tiled=False, axis_index_groups=groups)], False


def swap(x, wide, mask):
    return lax.ppermute(x, "wide", [(d, d ^ mask) for d in range(wide)])


def slab_stage(parts, wide, inner, early, split):
    stack = parts[0] if len(parts) == 1 else jnp.concatenate(parts)
    if inner != 4:
        return [stack] + [swap(stack, wide, m) for m in range(1, inner)]
    if early and len(parts) > 1:
        across = [swap(parts[0], wide, 2)]
        if split and len(parts) > 2:
            chunks = [parts[1], jnp.concatenate(parts[2:])]
        else:
            chunks = [jnp.concatenate(parts[1:])]
        across += [swap(chunk, wide, 2) for chunk in chunks]
        if split:
            beside = [swap(stack, wide, 1)]
        else:
            beside = [swap(parts[0], wide, 1), swap(chunks[0], wide, 1)]
        return [stack] + beside + across + [swap(piece, wide, 1) for piece in across]
    across = swap(stack, wide, 2)
    return [stack, swap(stack, wide, 1), across, swap(across, wide, 1)]


def gather_blocks(x, wide, early, split=False):
    inner = inner_size(wide)
    lines = wide // inner
    parts, shifted = line_stage(x, wide, inner)
    pieces = slab_stage(parts, wide, inner, early, split)
    me = lax.axis_index("wide")
    line = np.arange(lines, dtype=np.int32)
    source_line = (me // inner - line) % lines if shifted else jnp.asarray(line)
    masks = np.arange(inner, dtype=np.int32)
    blocks = (
        source_line[None, :] * inner
        + jnp.bitwise_xor(me % inner, jnp.asarray(masks))[:, None]
    )
    return pieces, blocks.reshape(wide)


def tiles_by_lag(retarded_tiles, tile_lags, column_of_block, block_of_slot, lags_wanted):
    columns = jnp.take(column_of_block, block_of_slot, axis=0)
    tiles = jnp.take(retarded_tiles[0], columns, axis=0)
    lags = jnp.take(tile_lags[0], columns, axis=0)
    zero = jnp.zeros_like(tiles[:, 0])
    return jnp.stack(
        [
            jnp.where(
                (lags[:, 0] == lag)[:, None, None],
                tiles[:, 0],
                jnp.where((lags[:, 1] == lag)[:, None, None], tiles[:, 1], zero),
            )
            for lag in lags_wanted
        ],
        axis=1,
    )


def rowwise(tiles, currents):
    spec = "slpq,slpr->qr" if tiles.ndim == 4 else "spq,spr->qr"
    return jnp.einsum(spec, tiles, currents, preferred_element_type=jnp.float32)


def per_device(wide, retarded_tiles, tile_lags, block_owner, later_current, excitation, inverse_blocks):
    lag_count = later_current.shape[0]
    step_count = excitation.shape[0]
    column_of_block = jnp.argsort(block_owner)

    later, later_blocks = gather_blocks(later_current, wide, True, split=True)
    offsets = np.cumsum([0] + [piece.shape[0] for piece in later])
    by_lag = tiles_by_lag(
        retarded_tiles, tile_lags, column_of_block, later_blocks, range(1, lag_count + 1)
    )
    inverse_t = inverse_blocks[0].T

    def advance(moment, retarded):
        source = excitation[moment] - retarded
        return with_layout_constraint(jnp.dot(
            inverse_t, source, precision=lax.Precision.HIGHEST, preferred_element_type=jnp.float32
        ), Layout((0, 1)))

    results = [None] * step_count
    newer = {}
    recent = None
    for moment in range(step_count - 1, -1, -1):
        first = max(1, step_count - moment)
        retarded = None
        for m, piece in enumerate(later):
            term = rowwise(
                by_lag[offsets[m] : offsets[m + 1], first - 1 :],
                piece[:, moment + first - step_count : moment + lag_count + 1 - step_count],
            )
            retarded = term if retarded is None else retarded + term
        for delay in range(1, first):
            retarded = retarded + rowwise(recent[:, delay - 1], newer[moment + delay])
        current = advance(moment, retarded)
        results[moment] = current
        if moment > 0:
            pieces, new_blocks = gather_blocks(current.astype(jnp.bfloat16), wide, True)
            newer[moment] = jnp.concatenate(pieces)
            if recent is None:
                recent = tiles_by_lag(
                    retarded_tiles,
                    tile_lags,
                    column_of_block,
                    new_blocks,
                    range(1, min(lag_count, step_count - 1) + 1),
                )
    return jnp.stack(results)


def solution(mesh):
    in_specs = (
        P(("groups", "wide"), None, None, None, None),
        P(("groups", "wide"), None, None),
        P("groups"),
        P(None, ("groups", "wide"), None),
        P(None, ("groups", "wide"), None),
        P(("groups", "wide"), None, None),
    )
    out_specs = P(None, ("groups", "wide"), None)
    return jax.shard_map(
        functools.partial(per_device, mesh.shape["wide"]),
        mesh=mesh,
        in_specs=in_specs,
        out_specs=out_specs,
        check_vma=False,
    )
```
